128 devices in a mesh: tm: 8 (over y, core), neuron: 8 (over x, z_hi), motif: 2 (over z_lo).
Axes of the slice: x: 4, y: 4, z: 4 (z_hi: 2, z_lo: 2; z = z_hi * 2 + z_lo), core: 2. Of those that a mesh axis runs over, the one named last changes fastest.
Arguments:
- counts: int32 [2048, 8192], P('neuron', 'tm'), may hold values from 0 to 2
- motif_w: float32 [64, 64, 2048], P('motif', None, 'neuron'), may hold values from 0.05 to 3, as said below
- motif_h: float32 [64, 8192], P('motif', 'tm'), may hold values from 0.05 to 3, as said below
Outputs:
- new_w: float32 [64, 64, 2048], P('motif', None, 'neuron')
- new_h: float32 [64, 8192], P('motif', 'tm')
The draws below stay inside these ranges and needn't reach their ends.
Inputs may be any that keep to these rules, and one draw needn't show every extreme that they name: `motif_w`: positive factors. `motif_h`: positive activations.
All inputs are finite; a program needn't handle non-finite values.
Results may differ from the reference program's by a relative error of at most 0.0003.
Values may be sent and summed in bfloat16 or wider, within the bound.
No kernel may reach another device: no remote copies, remote signals or barrier semaphores. Data moves between devices by JAX's collectives and lax.ppermute only.
A program may use at most 128 MiB of HBM per device.

```python
import jax
import jax.numpy as jnp
from jax import lax

MOTIFS = 64
LAGS = 64
NEUR_DEV = 256
BIN_DEV = 1024
ITERS = 2
NEURONS = 2048
TBINS = 8192


def strong_values(key, shape):
    base = jax.random.uniform(key, shape, jnp.float32)
    return 0.5 * jnp.exp(jnp.log(6.0) * base)


def draw_motif_w(key, part):
    values = strong_values(jax.random.fold_in(key, 11), (MOTIFS, LAGS, NEURONS))
    group = jnp.arange(MOTIFS, dtype=jnp.int32) // (MOTIFS // 2) % 2
    block = jnp.arange(NEURONS, dtype=jnp.int32) // NEUR_DEV % 2
    strong = group[:, None, None] == block[None, None, :]
    return jnp.where(strong, values, 0.1 * values).astype(jnp.float32)


def draw_motif_h(key, part):
    values = strong_values(jax.random.fold_in(key, 23), (MOTIFS, TBINS))
    group = jnp.arange(MOTIFS, dtype=jnp.int32) // (MOTIFS // 2) % 2
    block = jnp.arange(TBINS, dtype=jnp.int32) // BIN_DEV % 2
    strong = group[:, None] != block[None, :]
    return jnp.where(strong, values, 0.1 * values).astype(jnp.float32)


def place_ends(array, own_key, low, high):
    shape = array.shape
    index_at = [jax.random.randint(jax.random.fold_in(own_key, axis), (), 0, shape[axis]) for axis in range(len(shape))]
    array = array.at[tuple(index_at)].set(low)
    longest = shape.index(max(shape))
    index_at[longest] = (index_at[longest] + 1) % shape[longest]
    return array.at[tuple(index_at)].set(high)


def setup_inputs(seed: int = 0) -> dict:
    key_list = jax.random.split(jax.random.key(seed), 4)
    return {
        "counts": place_ends(jax.random.randint(key_list[0], (NEURONS, TBINS), 0, 3), jax.random.fold_in(key_list[0], 1), 0, 2).astype(jnp.int32),
        "motif_w": draw_motif_w(jax.random.fold_in(key_list[3], 71), 0),
        "motif_h": draw_motif_h(jax.random.fold_in(key_list[3], 71), 0),
    }


def stacked(hext, count, rim, width):
    rows = [hext[:, rim - lag: rim - lag + width] for lag in range(rim + 1)]
    return jnp.stack(rows, axis=1).reshape(count * (rim + 1), width)


def reference(counts, motif_w, motif_h):
    rim = LAGS - 1
    scale_factor = 1.0 / (MOTIFS * LAGS)
    weights = motif_w.reshape(MOTIFS * LAGS, NEURONS)
    acts = motif_h
    spike_events = counts.astype(jnp.float32)
    reduce_over_rows = (((0,), (0,)), ((), ()))
    contract_cols = (((1,), (1,)), ((), ()))

    def extend_padded(acts):
        zeros = jnp.zeros((MOTIFS, rim), jnp.bfloat16)
        return jnp.concatenate([zeros, acts.astype(jnp.bfloat16)], axis=1)

    def ratio_of(weight_bfloat, lagged_copies):
        estimated_counts = lax.dot_general(weight_bfloat, lagged_copies, reduce_over_rows, preferred_element_type=jnp.float32) * scale_factor
        return (spike_events / estimated_counts).astype(jnp.bfloat16)

    bins = jnp.arange(TBINS, dtype=jnp.int32)
    offsets = jnp.arange(LAGS, dtype=jnp.int32)
    mask = ((bins[None, :] + offsets[:, None]) < TBINS).astype(jnp.float32)
    for step in range(ITERS):
        weight_bfloat = weights.astype(jnp.bfloat16)
        lagged_copies = stacked(extend_padded(acts), MOTIFS, rim, TBINS)
        ratio = ratio_of(weight_bfloat, lagged_copies)
        rext = jnp.concatenate([ratio, jnp.zeros((NEURONS, rim), jnp.bfloat16)], axis=1)
        prod = jnp.dot(weight_bfloat, rext, preferred_element_type=jnp.float32).reshape(MOTIFS, LAGS, TBINS + rim)
        hnum = jnp.zeros((MOTIFS, TBINS), jnp.float32)
        for lag in range(LAGS):
            hnum = hnum + prod[:, lag, lag:lag + TBINS]
        colsum = jnp.sum(weight_bfloat.astype(jnp.float32).reshape(MOTIFS, LAGS, NEURONS), axis=2)
        hden = jnp.dot(colsum, mask, precision=lax.Precision.HIGHEST)
        acts = acts * hnum / hden
        lagged_copies = stacked(extend_padded(acts), MOTIFS, rim, TBINS)
        ratio = ratio_of(weight_bfloat, lagged_copies)
        wnum = lax.dot_general(lagged_copies, ratio, contract_cols, preferred_element_type=jnp.float32)
        wden = jnp.sum(lagged_copies, axis=1, dtype=jnp.float32)
        weights = weights * wnum / wden[:, None]
    return weights.reshape(MOTIFS, LAGS, NEURONS), acts
```

```python
import jax
import jax.numpy as jnp
from jax import lax
from jax.sharding import PartitionSpec as P

MOTIFS = 64
LAGS = 64
ITERS = 2


def from_behind(value, axis, steps):
    count = lax.axis_size(axis)
    first, last = (max(0, -steps), min(count, count - steps))
    return lax.ppermute(value, axis, [(source, source + steps) for source in range(first, last)])


def xor_swap(value, axis, mask):
    count = lax.axis_size(axis)
    return lax.ppermute(value, axis, [(source, source ^ mask) for source in range(count)])


def masks_of(axis):
    count = lax.axis_size(axis)
    masks = []
    mask = 1
    while mask < count:
        masks.append(mask)
        mask *= 2
    return masks


def all_sum(value, axis):
    for mask in masks_of(axis):
        value = jax.tree.map(lambda a, b: a + b, value, xor_swap(value, axis, mask))
    return value


def bit_of(axis, mask):
    return (lax.axis_index(axis) // mask) % 2 == 1


def sum_scatter(value, axis):
    for mask in masks_of(axis):
        half = value.shape[0] // 2
        low, high = value[:half], value[half:]
        upper = bit_of(axis, mask)
        send = jnp.where(upper, low, high)
        keep = jnp.where(upper, high, low)
        value = keep + xor_swap(send, axis, mask)
    return value


def scatter_offset(axis, rows):
    offset = 0
    size = rows
    for mask in masks_of(axis):
        size //= 2
        offset = offset + jnp.where(bit_of(axis, mask), size, 0)
    return offset


def gather_rows(value, axis):
    for mask in reversed(masks_of(axis)):
        other = xor_swap(value, axis, mask)
        upper = bit_of(axis, mask)
        value = jnp.where(
            upper, jnp.concatenate([other, value], axis=0), jnp.concatenate([value, other], axis=0)
        )
    return value


def stacked(hext, count, rim, width):
    rows = [hext[:, rim - lag : rim - lag + width] for lag in range(rim + 1)]
    return jnp.stack(rows, axis=1).reshape(count * (rim + 1), width)


def local(counts, motif_w, motif_h):
    k_dev, lags, n_dev = motif_w.shape
    width = counts.shape[1]
    rim = lags - 1
    rows = k_dev * lags
    scale_factor = 1.0 / (MOTIFS * LAGS)
    total_bins = width * lax.axis_size("tm")
    leading_bin = lax.axis_index("tm") * width
    reduce_over_rows = (((0,), (0,)), ((), ()))
    contract_cols = (((1,), (1,)), ((), ()))
    spike_events = counts.astype(jnp.float32)
    weights = motif_w.reshape(rows, n_dev)
    weight_bfloat = weights.astype(jnp.bfloat16)
    acts = motif_h
    offset = scatter_offset("tm", rows)
    part_rows = rows // lax.axis_size("tm")
    weight_part = lax.dynamic_slice_in_dim(weights, offset, part_rows, axis=0)

    def extend_padded(acts):
        hbf = acts.astype(jnp.bfloat16)
        before = from_behind(hbf[:, width - rim :], "tm", 1)
        return jnp.concatenate([before, hbf], axis=1)

    def ratio_and_lagged(weight_bfloat, hext):
        lagged_copies = stacked(hext, k_dev, rim, width)
        part = (
            lax.dot_general(
                weight_bfloat, lagged_copies, reduce_over_rows, preferred_element_type=jnp.float32
            )
            * scale_factor
        )
        estimated_counts = part + xor_swap(part, "motif", 1)
        return ((spike_events / estimated_counts).astype(jnp.bfloat16), lagged_copies)

    bins = leading_bin + jnp.arange(width, dtype=jnp.int32)
    offsets = jnp.arange(lags, dtype=jnp.int32)
    mask = (bins[None, :] + offsets[:, None] < total_bins).astype(jnp.float32)
    hext = extend_padded(acts)
    for step in range(ITERS):
        ratio, lagged_copies = ratio_and_lagged(weight_bfloat, hext)
        after = from_behind(ratio[:, :rim], "tm", -1)
        rext = jnp.concatenate([ratio, after], axis=1)
        prod = jnp.dot(weight_bfloat, rext, preferred_element_type=jnp.float32).reshape(
            k_dev, lags, width + rim
        )
        hnum = jnp.zeros((k_dev, width), jnp.float32)
        for lag in range(lags):
            hnum = hnum + prod[:, lag, lag : lag + width]
        colsum = jnp.sum(weight_bfloat.reshape(k_dev, lags, n_dev), axis=2, dtype=jnp.float32)
        hnum, colsum = all_sum((hnum, colsum), "neuron")
        hden = jnp.dot(colsum, mask, precision=lax.Precision.HIGHEST)
        acts = acts * hnum / hden
        hext = extend_padded(acts)
        ratio, lagged_copies = ratio_and_lagged(weight_bfloat, hext)
        wnum = lax.dot_general(
            lagged_copies, ratio, contract_cols, preferred_element_type=jnp.float32
        )
        wden = jnp.sum(lagged_copies, axis=1, dtype=jnp.float32)
        wnum = sum_scatter(wnum, "tm")
        wden = all_sum(wden, "tm")
        wden_part = lax.dynamic_slice_in_dim(wden, offset, part_rows, axis=0)
        weight_part = weight_part * wnum / wden_part[:, None]
        if step + 1 < ITERS:
            weight_bfloat = gather_rows(weight_part.astype(jnp.bfloat16), "tm")
    weights = gather_rows(weight_part, "tm")
    return (weights.reshape(k_dev, lags, n_dev), acts)


def solution(mesh):
    in_specs = (P("neuron", "tm"), P("motif", None, "neuron"), P("motif", "tm"))
    out_specs = (P("motif", None, "neuron"), P("motif", "tm"))
    return jax.shard_map(local, mesh=mesh, in_specs=in_specs, out_specs=out_specs, check_vma=False)
```

```python
import jax
import jax.numpy as jnp
from jax import lax
from jax.sharding import PartitionSpec as P

MOTIFS = 64
LAGS = 64
ITERS = 2


def from_behind(value, axis, steps):
    count = lax.axis_size(axis)
    first, last = (max(0, -steps), min(count, count - steps))
    return lax.ppermute(value, axis, [(source, source + steps) for source in range(first, last)])


def xor_swap(value, axis, mask):
    count = lax.axis_size(axis)
    return lax.ppermute(value, axis, [(source, source ^ mask) for source in range(count)])


def masks_of(axis):
    count = lax.axis_size(axis)
    masks = []
    mask = 1
    while mask < count:
        masks.append(mask)
        mask *= 2
    return masks


def all_sum(value, axis):
    for mask in masks_of(axis):
        value = jax.tree.map(lambda a, b: a + b, value, xor_swap(value, axis, mask))
    return value


def bit_of(axis, mask):
    return (lax.axis_index(axis) // mask) % 2 == 1


def sum_scatter(value, axis):
    for mask in masks_of(axis):
        half = value.shape[0] // 2
        low, high = value[:half], value[half:]
        upper = bit_of(axis, mask)
        send = jnp.where(upper, low, high)
        keep = jnp.where(upper, high, low)
        value = keep + xor_swap(send, axis, mask)
    return value


def scatter_offset(axis, rows):
    offset = 0
    size = rows
    for mask in masks_of(axis):
        size //= 2
        offset = offset + jnp.where(bit_of(axis, mask), size, 0)
    return offset


def gather_rows(value, axis):
    for mask in reversed(masks_of(axis)):
        other = xor_swap(value, axis, mask)
        upper = bit_of(axis, mask)
        value = jnp.where(
            upper, jnp.concatenate([other, value], axis=0), jnp.concatenate([value, other], axis=0)
        )
    return value


CONV_DIMS = lax.ConvDimensionNumbers


def recon_of(weight_bfloat, hext):
    flipped = jnp.flip(weight_bfloat, axis=1)
    dims = CONV_DIMS((0, 1, 2), (2, 0, 1), (0, 1, 2))
    return lax.conv_general_dilated(
        hext[None], flipped, (1,), [(0, 0)], dimension_numbers=dims,
        preferred_element_type=jnp.float32,
    )[0]


def hnum_of(weight_bfloat, rext):
    dims = CONV_DIMS((0, 1, 2), (0, 2, 1), (0, 1, 2))
    return lax.conv_general_dilated(
        rext[None], weight_bfloat, (1,), [(0, 0)], dimension_numbers=dims,
        preferred_element_type=jnp.float32,
    )[0]


def wnum_of(hext, ratio):
    dims = CONV_DIMS((1, 0, 2), (1, 0, 2), (0, 2, 1))
    out = lax.conv_general_dilated(
        hext[None], ratio[None], (1,), [(0, 0)], dimension_numbers=dims,
        preferred_element_type=jnp.float32,
    )
    return jnp.flip(out, axis=1)


def local(counts, motif_w, motif_h):
    k_dev, lags, n_dev = motif_w.shape
    width = counts.shape[1]
    rim = lags - 1
    rows = k_dev * lags
    scale_factor = 1.0 / (MOTIFS * LAGS)
    total_bins = width * lax.axis_size("tm")
    leading_bin = lax.axis_index("tm") * width
    spike_events = counts.astype(jnp.float32)
    weights = motif_w.reshape(rows, n_dev)
    weight_bfloat = motif_w.astype(jnp.bfloat16)
    acts = motif_h
    offset = scatter_offset("tm", rows)
    part_rows = rows // lax.axis_size("tm")
    weight_part = lax.dynamic_slice_in_dim(weights, offset, part_rows, axis=0)
    place = jnp.arange(width + rim, dtype=jnp.int32)[:, None]
    lag_ids = jnp.arange(lags, dtype=jnp.int32)[None, :]
    window = ((place >= rim - lag_ids) & (place < rim - lag_ids + width)).astype(jnp.bfloat16)

    def extend_padded(acts):
        hbf = acts.astype(jnp.bfloat16)
        before = from_behind(hbf[:, width - rim :], "tm", 1)
        return jnp.concatenate([before, hbf], axis=1)

    def ratio_of(weight_bfloat, hext):
        part = recon_of(weight_bfloat, hext) * scale_factor
        estimated_counts = part + xor_swap(part, "motif", 1)
        return (spike_events / estimated_counts).astype(jnp.bfloat16)

    bins = leading_bin + jnp.arange(width, dtype=jnp.int32)
    offsets = jnp.arange(lags, dtype=jnp.int32)
    mask = (bins[None, :] + offsets[:, None] < total_bins).astype(jnp.float32)
    hext = extend_padded(acts)
    for step in range(ITERS):
        ratio = ratio_of(weight_bfloat, hext)
        after = from_behind(ratio[:, :rim], "tm", -1)
        rext = jnp.concatenate([ratio, after], axis=1)
        hnum = hnum_of(weight_bfloat, rext)
        colsum = jnp.sum(weight_bfloat, axis=2, dtype=jnp.float32)
        hnum, colsum = all_sum((hnum, colsum), "neuron")
        hden = jnp.dot(colsum, mask, precision=lax.Precision.HIGHEST)
        acts = acts * hnum / hden
        hext = extend_padded(acts)
        ratio = ratio_of(weight_bfloat, hext)
        wnum = wnum_of(hext, ratio).reshape(rows, n_dev)
        wden = jnp.dot(hext, window, preferred_element_type=jnp.float32).reshape(rows)
        wnum = sum_scatter(wnum, "tm")
        wden = all_sum(wden, "tm")
        wden_part = lax.dynamic_slice_in_dim(wden, offset, part_rows, axis=0)
        weight_part = weight_part * wnum / wden_part[:, None]
        if step + 1 < ITERS:
            weight_bfloat = gather_rows(weight_part.astype(jnp.bfloat16), "tm").reshape(
                k_dev, lags, n_dev
            )
    weights = gather_rows(weight_part, "tm")
    return (weights.reshape(k_dev, lags, n_dev), acts)


def solution(mesh):
    in_specs = (P("neuron", "tm"), P("motif", None, "neuron"), P("motif", "tm"))
    out_specs = (P("motif", None, "neuron"), P("motif", "tm"))
    return jax.shard_map(local, mesh=mesh, in_specs=in_specs, out_specs=out_specs, check_vma=False)
```

```python
import jax
import jax.numpy as jnp
from jax import lax
from jax.sharding import PartitionSpec as P

MOTIFS = 64
LAGS = 64
ITERS = 2


def from_behind(value, axis, steps):
    count = lax.axis_size(axis)
    first, last = (max(0, -steps), min(count, count - steps))
    return lax.ppermute(value, axis, [(source, source + steps) for source in range(first, last)])


def xor_swap(value, axis, mask):
    count = lax.axis_size(axis)
    return lax.ppermute(value, axis, [(source, source ^ mask) for source in range(count)])


def masks_of(axis):
    count = lax.axis_size(axis)
    masks = []
    mask = 1
    while mask < count:
        masks.append(mask)
        mask *= 2
    return masks


def all_sum(value, axis):
    for mask in masks_of(axis):
        value = jax.tree.map(lambda a, b: a + b, value, xor_swap(value, axis, mask))
    return value


def bit_of(axis, mask):
    return (lax.axis_index(axis) // mask) % 2 == 1


def sum_scatter(value, axis):
    for mask in masks_of(axis):
        half = value.shape[0] // 2
        low, high = value[:half], value[half:]
        upper = bit_of(axis, mask)
        send = jnp.where(upper, low, high)
        keep = jnp.where(upper, high, low)
        value = keep + xor_swap(send, axis, mask)
    return value


def scatter_offset(axis, rows):
    offset = 0
    size = rows
    for mask in masks_of(axis):
        size //= 2
        offset = offset + jnp.where(bit_of(axis, mask), size, 0)
    return offset


def gather_rows(value, axis, dim=0):
    for mask in reversed(masks_of(axis)):
        other = xor_swap(value, axis, mask)
        upper = bit_of(axis, mask)
        value = jnp.where(
            upper,
            jnp.concatenate([other, value], axis=dim),
            jnp.concatenate([value, other], axis=dim),
        )
    return value


def from_behind_other(value, steps):
    count = lax.axis_size("tm")
    pairs = [(2 * source + side, 2 * (source + steps) + 1 - side)
             for source in range(count - steps) for side in range(2)]
    return lax.ppermute(value, ("tm", "motif"), pairs)


CONV_DIMS = lax.ConvDimensionNumbers


def recon_of(weight_bfloat, hext):
    flipped = jnp.flip(weight_bfloat, axis=1)
    dims = CONV_DIMS((0, 1, 2), (2, 0, 1), (0, 1, 2))
    return lax.conv_general_dilated(
        hext[None], flipped, (1,), [(0, 0)], dimension_numbers=dims,
        preferred_element_type=jnp.float32,
    )[0]


def hnum_of(weight_bfloat, rext):
    dims = CONV_DIMS((0, 1, 2), (0, 2, 1), (0, 1, 2))
    return lax.conv_general_dilated(
        rext[None], weight_bfloat, (1,), [(0, 0)], dimension_numbers=dims,
        preferred_element_type=jnp.float32,
    )[0]


def wnum_of(hext, ratio):
    dims = CONV_DIMS((1, 0, 2), (1, 0, 2), (0, 2, 1))
    out = lax.conv_general_dilated(
        hext[None], ratio[None], (1,), [(0, 0)], dimension_numbers=dims,
        preferred_element_type=jnp.float32,
    )
    return jnp.flip(out, axis=1)


def local(counts, motif_w, motif_h):
    k_dev, lags, n_dev = motif_w.shape
    width = counts.shape[1]
    rim = lags - 1
    rows = k_dev * lags
    scale_factor = 1.0 / (MOTIFS * LAGS)
    total_bins = width * lax.axis_size("tm")
    leading_bin = lax.axis_index("tm") * width
    spike_events = counts.astype(jnp.float32)
    weights = motif_w.reshape(rows, n_dev)
    weight_bfloat = motif_w.astype(jnp.bfloat16)
    weight_all = jnp.concatenate([weight_bfloat, xor_swap(weight_bfloat, "motif", 1)], axis=0)
    acts = motif_h
    offset = scatter_offset("tm", rows)
    part_rows = rows // lax.axis_size("tm")
    weight_part = lax.dynamic_slice_in_dim(weights, offset, part_rows, axis=0)
    place = jnp.arange(width + rim, dtype=jnp.int32)[:, None]
    lag_ids = jnp.arange(lags, dtype=jnp.int32)[None, :]
    window = ((place >= rim - lag_ids) & (place < rim - lag_ids + width)).astype(jnp.bfloat16)

    def extend_padded(acts):
        hbf = acts.astype(jnp.bfloat16)
        tail = hbf[:, width - rim :]
        own = jnp.concatenate([from_behind(tail, "tm", 1), hbf], axis=1)
        other = jnp.concatenate(
            [from_behind_other(tail, 1), xor_swap(hbf, "motif", 1)], axis=1
        )
        return own, jnp.concatenate([own, other], axis=0)

    def ratio_of(weight_all, hext_all):
        estimated_counts = recon_of(weight_all, hext_all) * scale_factor
        return (spike_events / estimated_counts).astype(jnp.bfloat16)

    bins = leading_bin + jnp.arange(width, dtype=jnp.int32)
    offsets = jnp.arange(lags, dtype=jnp.int32)
    mask = (bins[None, :] + offsets[:, None] < total_bins).astype(jnp.float32)
    hext, hext_all = extend_padded(acts)
    for step in range(ITERS):
        ratio = ratio_of(weight_all, hext_all)
        after = from_behind(ratio[:, :rim], "tm", -1)
        rext = jnp.concatenate([ratio, after], axis=1)
        hnum = hnum_of(weight_bfloat, rext)
        colsum = jnp.sum(weight_bfloat, axis=2, dtype=jnp.float32)
        hnum, colsum = all_sum((hnum, colsum), "neuron")
        hden = jnp.dot(colsum, mask, precision=lax.Precision.HIGHEST)
        acts = acts * hnum / hden
        hext, hext_all = extend_padded(acts)
        ratio = ratio_of(weight_all, hext_all)
        wnum = wnum_of(hext, ratio).reshape(rows, n_dev)
        wden = jnp.dot(hext, window, preferred_element_type=jnp.float32).reshape(rows)
        wnum = sum_scatter(wnum, "tm")
        wden = all_sum(wden, "tm")
        wden_part = lax.dynamic_slice_in_dim(wden, offset, part_rows, axis=0)
        weight_part = weight_part * wnum / wden_part[:, None]
        if step + 1 < ITERS:
            part_bfloat = weight_part.astype(jnp.bfloat16)
            pair = jnp.stack([part_bfloat, xor_swap(part_bfloat, "motif", 1)], axis=0)
            pair = gather_rows(pair, "tm", dim=1)
            weight_all = pair.reshape(2 * k_dev, lags, n_dev)
            weight_bfloat = weight_all[:k_dev]
    weights = gather_rows(weight_part, "tm")
    return (weights.reshape(k_dev, lags, n_dev), acts)


def solution(mesh):
    in_specs = (P("neuron", "tm"), P("motif", None, "neuron"), P("motif", "tm"))
    out_specs = (P("motif", None, "neuron"), P("motif", "tm"))
    return jax.shard_map(local, mesh=mesh, in_specs=in_specs, out_specs=out_specs, check_vma=False)
```

```python
import jax
import jax.numpy as jnp
from jax import lax
from jax.sharding import PartitionSpec as P

MOTIFS = 64
LAGS = 64
ITERS = 2


def from_behind(value, axis, steps):
    count = lax.axis_size(axis)
    first, last = (max(0, -steps), min(count, count - steps))
    return lax.ppermute(value, axis, [(source, source + steps) for source in range(first, last)])


def xor_swap(value, axis, mask):
    count = lax.axis_size(axis)
    return lax.ppermute(value, axis, [(source, source ^ mask) for source in range(count)])


def masks_of(axis):
    count = lax.axis_size(axis)
    masks = []
    mask = 1
    while mask < count:
        masks.append(mask)
        mask *= 2
    return masks


def all_sum(value, axis):
    for mask in masks_of(axis):
        value = jax.tree.map(lambda a, b: a + b, value, xor_swap(value, axis, mask))
    return value


def bit_of(axis, mask):
    return (lax.axis_index(axis) // mask) % 2 == 1


def sum_scatter(value, axis):
    for mask in masks_of(axis):
        half = value.shape[0] // 2
        low, high = value[:half], value[half:]
        upper = bit_of(axis, mask)
        send = jnp.where(upper, low, high)
        keep = jnp.where(upper, high, low)
        value = keep + xor_swap(send, axis, mask)
    return value


def scatter_offset(axis, rows):
    offset = 0
    size = rows
    for mask in masks_of(axis):
        size //= 2
        offset = offset + jnp.where(bit_of(axis, mask), size, 0)
    return offset


def gather_rows(value, axis, dim=0):
    for mask in reversed(masks_of(axis)):
        other = xor_swap(value, axis, mask)
        upper = bit_of(axis, mask)
        value = jnp.where(
            upper,
            jnp.concatenate([other, value], axis=dim),
            jnp.concatenate([value, other], axis=dim),
        )
    return value


def from_behind_other(value, steps):
    count = lax.axis_size("tm")
    pairs = [(2 * source + side, 2 * (source + steps) + 1 - side)
             for source in range(count - steps) for side in range(2)]
    return lax.ppermute(value, ("tm", "motif"), pairs)


def spread_sum(value, axis):
    count = lax.axis_size(axis)
    parts = value.reshape(count, value.shape[0] // count, *value.shape[1:])
    return jnp.sum(lax.all_to_all(parts, axis, 0, 0, tiled=True), axis=0)


def spread_gather(value, axis):
    count = lax.axis_size(axis)
    copies = jnp.broadcast_to(value[None], (count, *value.shape))
    gathered = lax.all_to_all(copies, axis, 0, 0, tiled=True)
    return gathered.reshape(count * value.shape[0], *value.shape[1:])


def full_sum(value, axis):
    count = lax.axis_size(axis)
    copies = jnp.broadcast_to(value[None], (count, *value.shape))
    return jnp.sum(lax.all_to_all(copies, axis, 0, 0, tiled=True), axis=0)


CONV_DIMS = lax.ConvDimensionNumbers


def recon_of(weight_bfloat, hext):
    flipped = jnp.flip(weight_bfloat, axis=1)
    dims = CONV_DIMS((0, 1, 2), (2, 0, 1), (0, 1, 2))
    return lax.conv_general_dilated(
        hext[None], flipped, (1,), [(0, 0)], dimension_numbers=dims,
        preferred_element_type=jnp.float32,
    )[0]


def hnum_of(weight_bfloat, rext):
    dims = CONV_DIMS((0, 1, 2), (0, 2, 1), (0, 1, 2))
    return lax.conv_general_dilated(
        rext[None], weight_bfloat, (1,), [(0, 0)], dimension_numbers=dims,
        preferred_element_type=jnp.float32,
    )[0]


def wnum_of(hext, ratio):
    dims = CONV_DIMS((1, 0, 2), (1, 0, 2), (0, 2, 1))
    out = lax.conv_general_dilated(
        hext[None], ratio[None], (1,), [(0, 0)], dimension_numbers=dims,
        preferred_element_type=jnp.float32,
    )
    return jnp.flip(out, axis=1)


def local(counts, motif_w, motif_h):
    k_dev, lags, n_dev = motif_w.shape
    width = counts.shape[1]
    rim = lags - 1
    rows = k_dev * lags
    scale_factor = 1.0 / (MOTIFS * LAGS)
    total_bins = width * lax.axis_size("tm")
    leading_bin = lax.axis_index("tm") * width
    spike_events = counts.astype(jnp.float32)
    weights = motif_w.reshape(rows, n_dev)
    weight_bfloat = motif_w.astype(jnp.bfloat16)
    weight_all = jnp.concatenate([weight_bfloat, xor_swap(weight_bfloat, "motif", 1)], axis=0)
    acts = motif_h
    part_rows = rows // lax.axis_size("tm")
    offset = lax.axis_index("tm") * part_rows
    weight_part = lax.dynamic_slice_in_dim(weights, offset, part_rows, axis=0)
    place = jnp.arange(width + rim, dtype=jnp.int32)[:, None]
    lag_ids = jnp.arange(lags, dtype=jnp.int32)[None, :]
    window = ((place >= rim - lag_ids) & (place < rim - lag_ids + width)).astype(jnp.bfloat16)

    def extend_padded(acts):
        hbf = acts.astype(jnp.bfloat16)
        tail = hbf[:, width - rim :]
        own = jnp.concatenate([from_behind(tail, "tm", 1), hbf], axis=1)
        other = jnp.concatenate(
            [from_behind_other(tail, 1), xor_swap(hbf, "motif", 1)], axis=1
        )
        return own, jnp.concatenate([own, other], axis=0)

    def ratio_of(weight_all, hext_all):
        estimated_counts = recon_of(weight_all, hext_all) * scale_factor
        return (spike_events / estimated_counts).astype(jnp.bfloat16)

    bins = leading_bin + jnp.arange(width, dtype=jnp.int32)
    offsets = jnp.arange(lags, dtype=jnp.int32)
    mask = (bins[None, :] + offsets[:, None] < total_bins).astype(jnp.float32)
    hext, hext_all = extend_padded(acts)
    for step in range(ITERS):
        ratio = ratio_of(weight_all, hext_all)
        after = from_behind(ratio[:, :rim], "tm", -1)
        rext = jnp.concatenate([ratio, after], axis=1)
        hnum = hnum_of(weight_bfloat, rext)
        colsum = jnp.sum(weight_bfloat, axis=2, dtype=jnp.float32)
        joined = full_sum(jnp.concatenate([hnum, colsum], axis=1), "neuron")
        hnum, colsum = joined[:, :width], joined[:, width:]
        hden = jnp.dot(colsum, mask, precision=lax.Precision.HIGHEST)
        acts = acts * hnum / hden
        hext, hext_all = extend_padded(acts)
        ratio = ratio_of(weight_all, hext_all)
        wnum = wnum_of(hext, ratio).reshape(rows, n_dev)
        wden = jnp.dot(hext, window, preferred_element_type=jnp.float32).reshape(rows)
        wnum = spread_sum(wnum, "tm")
        wden_part = spread_sum(wden, "tm")
        weight_part = weight_part * wnum / wden_part[:, None]
        if step + 1 < ITERS:
            part_bfloat = weight_part.astype(jnp.bfloat16)
            pair = jnp.stack([part_bfloat, xor_swap(part_bfloat, "motif", 1)], axis=0)
            pair = spread_gather(jnp.swapaxes(pair, 0, 1), "tm")
            weight_all = jnp.swapaxes(pair, 0, 1).reshape(2 * k_dev, lags, n_dev)
            weight_bfloat = weight_all[:k_dev]
    weights = spread_gather(weight_part, "tm")
    return (weights.reshape(k_dev, lags, n_dev), acts)


def solution(mesh):
    in_specs = (P("neuron", "tm"), P("motif", None, "neuron"), P("motif", "tm"))
    out_specs = (P("motif", None, "neuron"), P("motif", "tm"))
    return jax.shard_map(local, mesh=mesh, in_specs=in_specs, out_specs=out_specs, check_vma=False)
```

```python
import jax
import jax.numpy as jnp
from jax import lax
from jax.sharding import PartitionSpec as P

MOTIFS = 64
LAGS = 64
ITERS = 2


def from_behind(value, axis, steps):
    count = lax.axis_size(axis)
    first, last = (max(0, -steps), min(count, count - steps))
    return lax.ppermute(value, axis, [(source, source + steps) for source in range(first, last)])


def xor_swap(value, axis, mask):
    count = lax.axis_size(axis)
    return lax.ppermute(value, axis, [(source, source ^ mask) for source in range(count)])


def masks_of(axis):
    count = lax.axis_size(axis)
    masks = []
    mask = 1
    while mask < count:
        masks.append(mask)
        mask *= 2
    return masks


def all_sum(value, axis):
    for mask in masks_of(axis):
        value = jax.tree.map(lambda a, b: a + b, value, xor_swap(value, axis, mask))
    return value


def bit_of(axis, mask):
    return (lax.axis_index(axis) // mask) % 2 == 1


def sum_scatter(value, axis):
    for mask in masks_of(axis):
        half = value.shape[0] // 2
        low, high = value[:half], value[half:]
        upper = bit_of(axis, mask)
        send = jnp.where(upper, low, high)
        keep = jnp.where(upper, high, low)
        value = keep + xor_swap(send, axis, mask)
    return value


def scatter_offset(axis, rows):
    offset = 0
    size = rows
    for mask in masks_of(axis):
        size //= 2
        offset = offset + jnp.where(bit_of(axis, mask), size, 0)
    return offset


def gather_rows(value, axis, dim=0):
    for mask in reversed(masks_of(axis)):
        other = xor_swap(value, axis, mask)
        upper = bit_of(axis, mask)
        value = jnp.where(
            upper,
            jnp.concatenate([other, value], axis=dim),
            jnp.concatenate([value, other], axis=dim),
        )
    return value


def from_behind_other(value, steps):
    count = lax.axis_size("tm")
    pairs = [(2 * source + side, 2 * (source + steps) + 1 - side)
             for source in range(count - steps) for side in range(2)]
    return lax.ppermute(value, ("tm", "motif"), pairs)


CONV_DIMS = lax.ConvDimensionNumbers


def recon_of(weight_bfloat, hext):
    flipped = jnp.flip(weight_bfloat, axis=1)
    dims = CONV_DIMS((0, 1, 2), (2, 0, 1), (0, 1, 2))
    return lax.conv_general_dilated(
        hext[None], flipped, (1,), [(0, 0)], dimension_numbers=dims,
        preferred_element_type=jnp.float32,
    )[0]


def hnum_of(weight_bfloat, rext, chunk=16):
    k_dev, lags, n_dev = weight_bfloat.shape
    groups = lags // chunk
    width = rext.shape[1] - (lags - 1)
    grouped = weight_bfloat.reshape(k_dev * groups, chunk, n_dev)
    dims = CONV_DIMS((0, 1, 2), (0, 2, 1), (0, 1, 2))
    partial = lax.conv_general_dilated(
        rext[None], grouped, (1,), [(0, 0)], dimension_numbers=dims,
        preferred_element_type=jnp.float32,
    )[0].reshape(k_dev, groups, -1)
    total = partial[:, 0, :width]
    for group in range(1, groups):
        total = total + partial[:, group, chunk * group : chunk * group + width]
    return total


def wnum_of(hext, ratio, piece=16):
    k_dev, length = hext.shape
    n_dev, width = ratio.shape
    lags = length - width + 1
    pieces = width // piece
    spans = -(-(lags + piece) // piece)
    pad = (pieces + spans) * piece - length
    folded = jnp.pad(hext, ((0, 0), (0, pad))).reshape(k_dev, pieces + spans, piece)
    lhs = jnp.concatenate([folded[:, i : i + pieces, :] for i in range(spans)], axis=2)
    rhs = ratio.reshape(n_dev, pieces, piece)
    dims = CONV_DIMS((0, 1, 2), (0, 1, 2), (0, 2, 1))
    out = lax.conv_general_dilated(
        lhs, rhs, (1,), [(0, 0)], dimension_numbers=dims,
        preferred_element_type=jnp.float32,
    )
    return jnp.flip(out[:, :lags, :], axis=1)


def local(counts, motif_w, motif_h):
    k_dev, lags, n_dev = motif_w.shape
    width = counts.shape[1]
    rim = lags - 1
    rows = k_dev * lags
    scale_factor = 1.0 / (MOTIFS * LAGS)
    total_bins = width * lax.axis_size("tm")
    leading_bin = lax.axis_index("tm") * width
    spike_events = counts.astype(jnp.float32)
    weights = motif_w.reshape(rows, n_dev)
    weight_bfloat = motif_w.astype(jnp.bfloat16)
    weight_all = jnp.concatenate([weight_bfloat, xor_swap(weight_bfloat, "motif", 1)], axis=0)
    acts = motif_h
    offset = scatter_offset("tm", rows)
    part_rows = rows // lax.axis_size("tm")
    weight_part = lax.dynamic_slice_in_dim(weights, offset, part_rows, axis=0)
    place = jnp.arange(width + rim, dtype=jnp.int32)[:, None]
    lag_ids = jnp.arange(lags, dtype=jnp.int32)[None, :]
    window = ((place >= rim - lag_ids) & (place < rim - lag_ids + width)).astype(jnp.bfloat16)

    def extend_padded(acts):
        hbf = acts.astype(jnp.bfloat16)
        tail = hbf[:, width - rim :]
        own = jnp.concatenate([from_behind(tail, "tm", 1), hbf], axis=1)
        other = jnp.concatenate(
            [from_behind_other(tail, 1), xor_swap(hbf, "motif", 1)], axis=1
        )
        return own, jnp.concatenate([own, other], axis=0)

    def ratio_of(weight_all, hext_all):
        estimated_counts = recon_of(weight_all, hext_all) * scale_factor
        return (spike_events / estimated_counts).astype(jnp.bfloat16)

    bins = leading_bin + jnp.arange(width, dtype=jnp.int32)
    offsets = jnp.arange(lags, dtype=jnp.int32)
    mask = (bins[None, :] + offsets[:, None] < total_bins).astype(jnp.float32)
    hext, hext_all = extend_padded(acts)
    for step in range(ITERS):
        ratio = ratio_of(weight_all, hext_all)
        after = from_behind(ratio[:, :rim], "tm", -1)
        rext = jnp.concatenate([ratio, after], axis=1)
        hnum = hnum_of(weight_bfloat, rext)
        colsum = jnp.sum(weight_bfloat, axis=2, dtype=jnp.float32)
        hnum, colsum = all_sum((hnum, colsum), "neuron")
        hden = jnp.dot(colsum, mask, precision=lax.Precision.HIGHEST)
        acts = acts * hnum / hden
        hext, hext_all = extend_padded(acts)
        ratio = ratio_of(weight_all, hext_all)
        wnum = wnum_of(hext, ratio).reshape(rows, n_dev)
        wden = jnp.dot(hext, window, preferred_element_type=jnp.float32).reshape(rows)
        wnum = sum_scatter(wnum, "tm")
        wden = all_sum(wden, "tm")
        wden_part = lax.dynamic_slice_in_dim(wden, offset, part_rows, axis=0)
        weight_part = weight_part * wnum / wden_part[:, None]
        if step + 1 < ITERS:
            part_bfloat = weight_part.astype(jnp.bfloat16)
            pair = jnp.stack([part_bfloat, xor_swap(part_bfloat, "motif", 1)], axis=0)
            pair = gather_rows(pair, "tm", dim=1)
            weight_all = pair.reshape(2 * k_dev, lags, n_dev)
            weight_bfloat = weight_all[:k_dev]
    weights = gather_rows(weight_part, "tm")
    return (weights.reshape(k_dev, lags, n_dev), acts)


def solution(mesh):
    in_specs = (P("neuron", "tm"), P("motif", None, "neuron"), P("motif", "tm"))
    out_specs = (P("motif", None, "neuron"), P("motif", "tm"))
    return jax.shard_map(local, mesh=mesh, in_specs=in_specs, out_specs=out_specs, check_vma=False)
```

```python
import jax
import jax.numpy as jnp
from jax import lax
from jax.sharding import PartitionSpec as P

MOTIFS = 64
LAGS = 64
ITERS = 2


def from_behind(value, axis, steps):
    count = lax.axis_size(axis)
    first, last = (max(0, -steps), min(count, count - steps))
    return lax.ppermute(value, axis, [(source, source + steps) for source in range(first, last)])


def xor_swap(value, axis, mask):
    count = lax.axis_size(axis)
    return lax.ppermute(value, axis, [(source, source ^ mask) for source in range(count)])


def masks_of(axis):
    count = lax.axis_size(axis)
    masks = []
    mask = 1
    while mask < count:
        masks.append(mask)
        mask *= 2
    return masks


def all_sum(value, axis):
    for mask in masks_of(axis):
        value = jax.tree.map(lambda a, b: a + b, value, xor_swap(value, axis, mask))
    return value


def bit_of(axis, mask):
    return (lax.axis_index(axis) // mask) % 2 == 1


def sum_scatter(value, axis):
    for mask in masks_of(axis):
        half = value.shape[0] // 2
        low, high = value[:half], value[half:]
        upper = bit_of(axis, mask)
        send = jnp.where(upper, low, high)
        keep = jnp.where(upper, high, low)
        value = keep + xor_swap(send, axis, mask)
    return value


def scatter_offset(axis, rows):
    offset = 0
    size = rows
    for mask in masks_of(axis):
        size //= 2
        offset = offset + jnp.where(bit_of(axis, mask), size, 0)
    return offset


def gather_rows(value, axis, dim=0):
    for mask in reversed(masks_of(axis)):
        other = xor_swap(value, axis, mask)
        upper = bit_of(axis, mask)
        value = jnp.where(
            upper,
            jnp.concatenate([other, value], axis=dim),
            jnp.concatenate([value, other], axis=dim),
        )
    return value


def from_behind_other(value, steps):
    count = lax.axis_size("tm")
    pairs = [(2 * source + side, 2 * (source + steps) + 1 - side)
             for source in range(count - steps) for side in range(2)]
    return lax.ppermute(value, ("tm", "motif"), pairs)


def spread_sum(value, axis):
    count = lax.axis_size(axis)
    parts = value.reshape(count, value.shape[0] // count, *value.shape[1:])
    return jnp.sum(lax.all_to_all(parts, axis, 0, 0, tiled=True), axis=0)


def spread_gather(value, axis):
    count = lax.axis_size(axis)
    copies = jnp.broadcast_to(value[None], (count, *value.shape))
    gathered = lax.all_to_all(copies, axis, 0, 0, tiled=True)
    return gathered.reshape(count * value.shape[0], *value.shape[1:])


CONV_DIMS = lax.ConvDimensionNumbers


def recon_of(weight_bfloat, hext):
    flipped = jnp.flip(weight_bfloat, axis=1)
    dims = CONV_DIMS((0, 1, 2), (2, 0, 1), (0, 1, 2))
    return lax.conv_general_dilated(
        hext[None], flipped, (1,), [(0, 0)], dimension_numbers=dims,
        preferred_element_type=jnp.float32,
    )[0]


def hnum_of(weight_bfloat, rext, chunk=16):
    k_dev, lags, n_dev = weight_bfloat.shape
    groups = lags // chunk
    width = rext.shape[1] - (lags - 1)
    grouped = weight_bfloat.reshape(k_dev * groups, chunk, n_dev)
    dims = CONV_DIMS((0, 1, 2), (0, 2, 1), (0, 1, 2))
    partial = lax.conv_general_dilated(
        rext[None], grouped, (1,), [(0, 0)], dimension_numbers=dims,
        preferred_element_type=jnp.float32,
    )[0].reshape(k_dev, groups, -1)
    total = partial[:, 0, :width]
    for group in range(1, groups):
        total = total + partial[:, group, chunk * group : chunk * group + width]
    return total


def wnum_of(hext, ratio, piece=16):
    k_dev, length = hext.shape
    n_dev, width = ratio.shape
    lags = length - width + 1
    pieces = width // piece
    spans = -(-(lags + piece) // piece)
    pad = (pieces + spans) * piece - length
    folded = jnp.pad(hext, ((0, 0), (0, pad))).reshape(k_dev, pieces + spans, piece)
    lhs = jnp.concatenate([folded[:, i : i + pieces, :] for i in range(spans)], axis=2)
    rhs = ratio.reshape(n_dev, pieces, piece)
    dims = CONV_DIMS((0, 1, 2), (0, 1, 2), (0, 2, 1))
    out = lax.conv_general_dilated(
        lhs, rhs, (1,), [(0, 0)], dimension_numbers=dims,
        preferred_element_type=jnp.float32,
    )
    return jnp.flip(out[:, :lags, :], axis=1)


def local(counts, motif_w, motif_h):
    k_dev, lags, n_dev = motif_w.shape
    width = counts.shape[1]
    rim = lags - 1
    rows = k_dev * lags
    scale_factor = 1.0 / (MOTIFS * LAGS)
    total_bins = width * lax.axis_size("tm")
    leading_bin = lax.axis_index("tm") * width
    spike_events = counts.astype(jnp.float32)
    weights = motif_w.reshape(rows, n_dev)
    weight_bfloat = motif_w.astype(jnp.bfloat16)
    weight_all = jnp.concatenate([weight_bfloat, xor_swap(weight_bfloat, "motif", 1)], axis=0)
    acts = motif_h
    offset = scatter_offset("tm", rows)
    part_rows = rows // lax.axis_size("tm")
    weight_part = lax.dynamic_slice_in_dim(weights, offset, part_rows, axis=0)
    place = jnp.arange(width + rim, dtype=jnp.int32)[:, None]
    lag_ids = jnp.arange(lags, dtype=jnp.int32)[None, :]
    window = ((place >= rim - lag_ids) & (place < rim - lag_ids + width)).astype(jnp.bfloat16)

    def extend_padded(acts):
        hbf = acts.astype(jnp.bfloat16)
        tail = hbf[:, width - rim :]
        own = jnp.concatenate([from_behind(tail, "tm", 1), hbf], axis=1)
        other = jnp.concatenate(
            [from_behind_other(tail, 1), xor_swap(hbf, "motif", 1)], axis=1
        )
        return own, jnp.concatenate([own, other], axis=0)

    def ratio_of(weight_all, hext_all):
        estimated_counts = recon_of(weight_all, hext_all) * scale_factor
        return (spike_events / estimated_counts).astype(jnp.bfloat16)

    bins = leading_bin + jnp.arange(width, dtype=jnp.int32)
    offsets = jnp.arange(lags, dtype=jnp.int32)
    mask = (bins[None, :] + offsets[:, None] < total_bins).astype(jnp.float32)
    hext, hext_all = extend_padded(acts)
    for step in range(ITERS):
        ratio = ratio_of(weight_all, hext_all)
        after = from_behind(ratio[:, :rim], "tm", -1)
        rext = jnp.concatenate([ratio, after], axis=1)
        hnum = hnum_of(weight_bfloat, rext)
        colsum = jnp.sum(weight_bfloat, axis=2, dtype=jnp.float32)
        joined = spread_gather(spread_sum(jnp.concatenate([hnum, colsum], axis=1), "neuron"), "neuron")
        hnum, colsum = joined[:, :width], joined[:, width:]
        hden = jnp.dot(colsum, mask, precision=lax.Precision.HIGHEST)
        acts = acts * hnum / hden
        hext, hext_all = extend_padded(acts)
        ratio = ratio_of(weight_all, hext_all)
        wnum = wnum_of(hext, ratio).reshape(rows, n_dev)
        wden = jnp.dot(hext, window, preferred_element_type=jnp.float32).reshape(rows)
        blocks = lax.axis_size("tm")
        joined = jnp.concatenate(
            [wnum.reshape(blocks, part_rows, n_dev), wden.reshape(blocks, 1, part_rows)], axis=1
        )
        joined = sum_scatter(joined, "tm")[0]
        wnum, wden_part = joined[:part_rows], joined[part_rows]
        weight_part = weight_part * wnum / wden_part[:, None]
        if step + 1 < ITERS:
            part_bfloat = weight_part.astype(jnp.bfloat16)
            pair = jnp.stack([part_bfloat, xor_swap(part_bfloat, "motif", 1)], axis=0)
            pair = gather_rows(pair, "tm", dim=1)
            weight_all = pair.reshape(2 * k_dev, lags, n_dev)
            weight_bfloat = weight_all[:k_dev]
    weights = gather_rows(weight_part, "tm")
    return (weights.reshape(k_dev, lags, n_dev), acts)


def solution(mesh):
    in_specs = (P("neuron", "tm"), P("motif", None, "neuron"), P("motif", "tm"))
    out_specs = (P("motif", None, "neuron"), P("motif", "tm"))
    return jax.shard_map(local, mesh=mesh, in_specs=in_specs, out_specs=out_specs, check_vma=False)
```

```python
import jax
import jax.numpy as jnp
from jax import lax
from jax.sharding import PartitionSpec as P

MOTIFS = 64
LAGS = 64
ITERS = 2


def from_behind(value, axis, steps):
    count = lax.axis_size(axis)
    first, last = (max(0, -steps), min(count, count - steps))
    return lax.ppermute(value, axis, [(source, source + steps) for source in range(first, last)])


def xor_swap(value, axis, mask):
    count = lax.axis_size(axis)
    return lax.ppermute(value, axis, [(source, source ^ mask) for source in range(count)])


def masks_of(axis):
    count = lax.axis_size(axis)
    masks = []
    mask = 1
    while mask < count:
        masks.append(mask)
        mask *= 2
    return masks


def all_sum(value, axis):
    for mask in masks_of(axis):
        value = jax.tree.map(lambda a, b: a + b, value, xor_swap(value, axis, mask))
    return value


def ring_steps(axis):
    count = lax.axis_size(axis)
    if count != 8:
        return [
            ([source ^ mask for source in range(count)],
             [(source // mask) % 2 == 1 for source in range(count)])
            for mask in masks_of(axis)
        ]
    steps = [([source ^ 1 for source in range(8)], [source % 2 == 1 for source in range(8)])]
    for flip in (0, 1):
        partners, uppers = [], []
        for source in range(8):
            row, core = divmod(source, 2)
            if core == flip:
                other, upper = row ^ 1, row in (1, 2)
            else:
                other, upper = 3 - row, row in (2, 3)
            partners.append(2 * other + core)
            uppers.append(upper)
        steps.append((partners, uppers))
    return steps


def swap_with(value, axis, partners):
    return lax.ppermute(value, axis, [(source, target) for source, target in enumerate(partners)])


def upper_of(axis, uppers):
    return jnp.asarray(uppers)[lax.axis_index(axis)]


def sum_scatter(value, axis):
    for partners, uppers in ring_steps(axis):
        half = value.shape[0] // 2
        low, high = value[:half], value[half:]
        upper = upper_of(axis, uppers)
        send = jnp.where(upper, low, high)
        keep = jnp.where(upper, high, low)
        value = keep + swap_with(send, axis, partners)
    return value


def scatter_offset(axis, rows):
    offset = 0
    size = rows
    for partners, uppers in ring_steps(axis):
        size //= 2
        offset = offset + jnp.where(upper_of(axis, uppers), size, 0)
    return offset


def gather_rows(value, axis, dim=0):
    for partners, uppers in reversed(ring_steps(axis)):
        other = swap_with(value, axis, partners)
        upper = upper_of(axis, uppers)
        value = jnp.where(
            upper,
            jnp.concatenate([other, value], axis=dim),
            jnp.concatenate([value, other], axis=dim),
        )
    return value


def from_behind_other(value, steps):
    count = lax.axis_size("tm")
    pairs = [(2 * source + side, 2 * (source + steps) + 1 - side)
             for source in range(count - steps) for side in range(2)]
    return lax.ppermute(value, ("tm", "motif"), pairs)


CONV_DIMS = lax.ConvDimensionNumbers


def recon_of(weight_bfloat, hext):
    flipped = jnp.flip(weight_bfloat, axis=1)
    dims = CONV_DIMS((0, 1, 2), (2, 0, 1), (0, 1, 2))
    return lax.conv_general_dilated(
        hext[None], flipped, (1,), [(0, 0)], dimension_numbers=dims,
        preferred_element_type=jnp.float32,
    )[0]


def hnum_of(weight_bfloat, rext, chunk=16):
    k_dev, lags, n_dev = weight_bfloat.shape
    groups = lags // chunk
    width = rext.shape[1] - (lags - 1)
    grouped = weight_bfloat.reshape(k_dev * groups, chunk, n_dev)
    dims = CONV_DIMS((0, 1, 2), (0, 2, 1), (0, 1, 2))
    partial = lax.conv_general_dilated(
        rext[None], grouped, (1,), [(0, 0)], dimension_numbers=dims,
        preferred_element_type=jnp.float32,
    )[0].reshape(k_dev, groups, -1)
    total = partial[:, 0, :width]
    for group in range(1, groups):
        total = total + partial[:, group, chunk * group : chunk * group + width]
    return total


def wnum_of(hext, ratio, piece=16):
    k_dev, length = hext.shape
    n_dev, width = ratio.shape
    lags = length - width + 1
    pieces = width // piece
    spans = -(-(lags + piece) // piece)
    pad = (pieces + spans) * piece - length
    folded = jnp.pad(hext, ((0, 0), (0, pad))).reshape(k_dev, pieces + spans, piece)
    lhs = jnp.concatenate([folded[:, i : i + pieces, :] for i in range(spans)], axis=2)
    rhs = ratio.reshape(n_dev, pieces, piece)
    dims = CONV_DIMS((0, 1, 2), (0, 1, 2), (0, 2, 1))
    out = lax.conv_general_dilated(
        lhs, rhs, (1,), [(0, 0)], dimension_numbers=dims,
        preferred_element_type=jnp.float32,
    )
    return jnp.flip(out[:, :lags, :], axis=1)


def local(counts, motif_w, motif_h):
    k_dev, lags, n_dev = motif_w.shape
    width = counts.shape[1]
    rim = lags - 1
    rows = k_dev * lags
    scale_factor = 1.0 / (MOTIFS * LAGS)
    total_bins = width * lax.axis_size("tm")
    leading_bin = lax.axis_index("tm") * width
    spike_events = counts.astype(jnp.float32)
    weights = motif_w.reshape(rows, n_dev)
    weight_bfloat = motif_w.astype(jnp.bfloat16)
    half_k = k_dev // 2
    second = lax.axis_index("tm") % 2 == 1
    mine = jnp.where(second, weight_bfloat[half_k:], weight_bfloat[:half_k])
    fetched = xor_swap(mine, "motif", 1)
    relayed = xor_swap(fetched, "tm", 1)
    partner_w = jnp.where(
        second,
        jnp.concatenate([relayed, fetched], axis=0),
        jnp.concatenate([fetched, relayed], axis=0),
    )
    weight_all = jnp.concatenate([weight_bfloat, partner_w], axis=0)
    acts = motif_h
    offset = scatter_offset("tm", rows)
    part_rows = rows // lax.axis_size("tm")
    weight_part = lax.dynamic_slice_in_dim(weights, offset, part_rows, axis=0)
    place = jnp.arange(width + rim, dtype=jnp.int32)[:, None]
    lag_ids = jnp.arange(lags, dtype=jnp.int32)[None, :]
    window = ((place >= rim - lag_ids) & (place < rim - lag_ids + width)).astype(jnp.bfloat16)

    def extend_padded(acts):
        hbf = acts.astype(jnp.bfloat16)
        tail = hbf[:, width - rim :]
        own = jnp.concatenate([from_behind(tail, "tm", 1), hbf], axis=1)
        other = jnp.concatenate(
            [from_behind_other(tail, 1), xor_swap(hbf, "motif", 1)], axis=1
        )
        return own, jnp.concatenate([own, other], axis=0)

    def ratio_of(weight_all, hext_all):
        estimated_counts = recon_of(weight_all, hext_all) * scale_factor
        return (spike_events / estimated_counts).astype(jnp.bfloat16)

    bins = leading_bin + jnp.arange(width, dtype=jnp.int32)
    offsets = jnp.arange(lags, dtype=jnp.int32)
    mask = (bins[None, :] + offsets[:, None] < total_bins).astype(jnp.float32)
    hext, hext_all = extend_padded(acts)
    for step in range(ITERS):
        ratio = ratio_of(weight_all, hext_all)
        after = from_behind(ratio[:, :rim], "tm", -1)
        rext = jnp.concatenate([ratio, after], axis=1)
        hnum = hnum_of(weight_bfloat, rext)
        colsum = jnp.sum(weight_bfloat, axis=2, dtype=jnp.float32)
        joined = all_sum(jnp.concatenate([hnum, colsum], axis=1), "neuron")
        hnum, colsum = joined[:, :width], joined[:, width:]
        hden = jnp.dot(colsum, mask, precision=lax.Precision.HIGHEST)
        acts = acts * hnum / hden
        hext, hext_all = extend_padded(acts)
        ratio = ratio_of(weight_all, hext_all)
        wnum = wnum_of(hext, ratio).reshape(rows, n_dev)
        wden = jnp.dot(hext, window, preferred_element_type=jnp.float32).reshape(rows)
        blocks = lax.axis_size("tm")
        joined = jnp.concatenate(
            [wnum.reshape(blocks, part_rows, n_dev), wden.reshape(blocks, 1, part_rows)], axis=1
        )
        joined = sum_scatter(joined, "tm")[0]
        wnum, wden_part = joined[:part_rows], joined[part_rows]
        weight_part = weight_part * wnum / wden_part[:, None]
        if step + 1 < ITERS:
            part_bfloat = weight_part.astype(jnp.bfloat16)
            pair = jnp.stack([part_bfloat, xor_swap(part_bfloat, "motif", 1)], axis=0)
            pair = gather_rows(pair, "tm", dim=1)
            weight_all = pair.reshape(2 * k_dev, lags, n_dev)
            weight_bfloat = weight_all[:k_dev]
    weights = gather_rows(weight_part, "tm")
    return (weights.reshape(k_dev, lags, n_dev), acts)


def solution(mesh):
    in_specs = (P("neuron", "tm"), P("motif", None, "neuron"), P("motif", "tm"))
    out_specs = (P("motif", None, "neuron"), P("motif", "tm"))
    return jax.shard_map(local, mesh=mesh, in_specs=in_specs, out_specs=out_specs, check_vma=False)
```

```python
import jax
import jax.numpy as jnp
from jax import lax
from jax.sharding import PartitionSpec as P

MOTIFS = 64
LAGS = 64
ITERS = 2


def from_behind(value, axis, steps):
    count = lax.axis_size(axis)
    first, last = (max(0, -steps), min(count, count - steps))
    return lax.ppermute(value, axis, [(source, source + steps) for source in range(first, last)])


def xor_swap(value, axis, mask):
    count = lax.axis_size(axis)
    return lax.ppermute(value, axis, [(source, source ^ mask) for source in range(count)])


def masks_of(axis):
    count = lax.axis_size(axis)
    masks = []
    mask = 1
    while mask < count:
        masks.append(mask)
        mask *= 2
    return masks


def all_sum(value, axis):
    for mask in masks_of(axis):
        value = jax.tree.map(lambda a, b: a + b, value, xor_swap(value, axis, mask))
    return value


def ring_steps(axis):
    count = lax.axis_size(axis)
    if count != 8:
        return [
            ([source ^ mask for source in range(count)],
             [(source // mask) % 2 == 1 for source in range(count)])
            for mask in masks_of(axis)
        ]
    steps = [([source ^ 1 for source in range(8)], [source % 2 == 1 for source in range(8)])]
    for flip in (0, 1):
        partners, uppers = [], []
        for source in range(8):
            row, core = divmod(source, 2)
            if core == flip:
                other, upper = row ^ 1, row in (1, 2)
            else:
                other, upper = 3 - row, row in (2, 3)
            partners.append(2 * other + core)
            uppers.append(upper)
        steps.append((partners, uppers))
    return steps


def swap_with(value, axis, partners):
    return lax.ppermute(value, axis, [(source, target) for source, target in enumerate(partners)])


def upper_of(axis, uppers):
    return jnp.asarray(uppers)[lax.axis_index(axis)]


def sum_scatter(value, axis):
    for partners, uppers in ring_steps(axis):
        half = value.shape[0] // 2
        upper = upper_of(axis, uppers)
        send = lax.dynamic_slice_in_dim(value, jnp.where(upper, 0, half), half, axis=0)
        keep = lax.dynamic_slice_in_dim(value, jnp.where(upper, half, 0), half, axis=0)
        value = keep + swap_with(send, axis, partners)
    return value


def scatter_offset(axis, rows):
    offset = 0
    size = rows
    for partners, uppers in ring_steps(axis):
        size //= 2
        offset = offset + jnp.where(upper_of(axis, uppers), size, 0)
    return offset


def gather_rows(value, axis, dim=0):
    steps = ring_steps(axis)
    run = value.shape[dim]
    total = run * 2 ** len(steps)
    start = scatter_offset(axis, total)
    shape = list(value.shape)
    shape[dim] = total
    full = lax.dynamic_update_slice_in_dim(jnp.zeros(shape, value.dtype), value, start, axis=dim)
    for partners, uppers in reversed(steps):
        upper = upper_of(axis, uppers)
        other = swap_with(value, axis, partners)
        other_start = jnp.where(upper, start - run, start + run)
        full = lax.dynamic_update_slice_in_dim(full, other, other_start, axis=dim)
        start = jnp.minimum(start, other_start)
        run *= 2
        if run < total:
            value = lax.dynamic_slice_in_dim(full, start, run, axis=dim)
    return full


def from_behind_other(value, steps):
    count = lax.axis_size("tm")
    pairs = [(2 * source + side, 2 * (source + steps) + 1 - side)
             for source in range(count - steps) for side in range(2)]
    return lax.ppermute(value, ("tm", "motif"), pairs)


CONV_DIMS = lax.ConvDimensionNumbers


def recon_of(weight_bfloat, hext):
    flipped = jnp.flip(weight_bfloat, axis=1)
    dims = CONV_DIMS((0, 1, 2), (2, 0, 1), (0, 1, 2))
    return lax.conv_general_dilated(
        hext[None], flipped, (1,), [(0, 0)], dimension_numbers=dims,
        preferred_element_type=jnp.float32,
    )[0]


def hnum_of(weight_bfloat, rext, chunk=16):
    k_dev, lags, n_dev = weight_bfloat.shape
    groups = lags // chunk
    width = rext.shape[1] - (lags - 1)
    grouped = weight_bfloat.reshape(k_dev * groups, chunk, n_dev)
    dims = CONV_DIMS((0, 1, 2), (0, 2, 1), (0, 1, 2))
    partial = lax.conv_general_dilated(
        rext[None], grouped, (1,), [(0, 0)], dimension_numbers=dims,
        preferred_element_type=jnp.float32,
    )[0].reshape(k_dev, groups, -1)
    total = partial[:, 0, :width]
    for group in range(1, groups):
        total = total + partial[:, group, chunk * group : chunk * group + width]
    return total


def wnum_of(hext, ratio, piece=32):
    k_dev, length = hext.shape
    n_dev, width = ratio.shape
    lags = length - width + 1
    pieces = width // piece
    spans = -(-(lags + piece) // piece)
    pad = (pieces + spans) * piece - length
    folded = jnp.pad(hext, ((0, 0), (0, pad))).reshape(k_dev, pieces + spans, piece)
    lhs = jnp.concatenate([folded[:, i : i + pieces, :] for i in range(spans)], axis=2)
    rhs = ratio.reshape(n_dev, pieces, piece)
    dims = CONV_DIMS((0, 1, 2), (0, 1, 2), (0, 2, 1))
    out = lax.conv_general_dilated(
        lhs, rhs, (1,), [(0, 0)], dimension_numbers=dims,
        preferred_element_type=jnp.float32,
    )
    return jnp.flip(out[:, :lags, :], axis=1)


def local(counts, motif_w, motif_h):
    k_dev, lags, n_dev = motif_w.shape
    width = counts.shape[1]
    rim = lags - 1
    rows = k_dev * lags
    scale_factor = 1.0 / (MOTIFS * LAGS)
    total_bins = width * lax.axis_size("tm")
    leading_bin = lax.axis_index("tm") * width
    spike_events = counts.astype(jnp.float32)
    weights = motif_w.reshape(rows, n_dev)
    weight_bfloat = motif_w.astype(jnp.bfloat16)
    half_k = k_dev // 2
    second = lax.axis_index("tm") % 2 == 1
    mine = jnp.where(second, weight_bfloat[half_k:], weight_bfloat[:half_k])
    fetched = xor_swap(mine, "motif", 1)
    relayed = xor_swap(fetched, "tm", 1)
    partner_w = jnp.where(
        second,
        jnp.concatenate([relayed, fetched], axis=0),
        jnp.concatenate([fetched, relayed], axis=0),
    )
    weight_all = jnp.concatenate([weight_bfloat, partner_w], axis=0)
    acts = motif_h
    offset = scatter_offset("tm", rows)
    part_rows = rows // lax.axis_size("tm")
    weight_part = lax.dynamic_slice_in_dim(weights, offset, part_rows, axis=0)
    place = jnp.arange(width + rim, dtype=jnp.int32)[:, None]
    lag_ids = jnp.arange(lags, dtype=jnp.int32)[None, :]
    window = ((place >= rim - lag_ids) & (place < rim - lag_ids + width)).astype(jnp.bfloat16)

    def extend_padded(acts):
        hbf = acts.astype(jnp.bfloat16)
        tail = hbf[:, width - rim :]
        own = jnp.concatenate([from_behind(tail, "tm", 1), hbf], axis=1)
        other = jnp.concatenate(
            [from_behind_other(tail, 1), xor_swap(hbf, "motif", 1)], axis=1
        )
        return own, jnp.concatenate([own, other], axis=0)

    def ratio_of(weight_all, hext_all):
        estimated_counts = recon_of(weight_all, hext_all) * scale_factor
        return (spike_events / estimated_counts).astype(jnp.bfloat16)

    bins = leading_bin + jnp.arange(width, dtype=jnp.int32)
    offsets = jnp.arange(lags, dtype=jnp.int32)
    mask = (bins[None, :] + offsets[:, None] < total_bins).astype(jnp.float32)
    hext, hext_all = extend_padded(acts)
    for step in range(ITERS):
        ratio = ratio_of(weight_all, hext_all)
        after = from_behind(ratio[:, :rim], "tm", -1)
        rext = jnp.concatenate([ratio, after], axis=1)
        hnum = hnum_of(weight_bfloat, rext)
        colsum = jnp.sum(weight_bfloat, axis=2, dtype=jnp.float32)
        joined = all_sum(jnp.concatenate([hnum, colsum], axis=1), "neuron")
        hnum, colsum = joined[:, :width], joined[:, width:]
        hden = jnp.dot(colsum, mask, precision=lax.Precision.HIGHEST)
        acts = acts * hnum / hden
        hext, hext_all = extend_padded(acts)
        ratio = ratio_of(weight_all, hext_all)
        wnum = wnum_of(hext, ratio).reshape(rows, n_dev)
        wden = jnp.dot(hext, window, preferred_element_type=jnp.float32).reshape(rows)
        blocks = lax.axis_size("tm")
        joined = jnp.concatenate(
            [wnum.reshape(blocks, part_rows, n_dev), wden.reshape(blocks, 1, part_rows)], axis=1
        )
        joined = sum_scatter(joined, "tm")[0]
        wnum, wden_part = joined[:part_rows], joined[part_rows]
        weight_part = weight_part * wnum / wden_part[:, None]
        if step + 1 < ITERS:
            part_bfloat = weight_part.astype(jnp.bfloat16)
            pair = jnp.stack([part_bfloat, xor_swap(part_bfloat, "motif", 1)], axis=0)
            pair = gather_rows(pair, "tm", dim=1)
            weight_all = pair.reshape(2 * k_dev, lags, n_dev)
            weight_bfloat = weight_all[:k_dev]
    weights = gather_rows(weight_part, "tm")
    return (weights.reshape(k_dev, lags, n_dev), acts)


def solution(mesh):
    in_specs = (P("neuron", "tm"), P("motif", None, "neuron"), P("motif", "tm"))
    out_specs = (P("motif", None, "neuron"), P("motif", "tm"))
    return jax.shard_map(local, mesh=mesh, in_specs=in_specs, out_specs=out_specs, check_vma=False)
```

```python
import jax
import jax.numpy as jnp
from jax import lax
from jax.sharding import PartitionSpec as P

MOTIFS = 64
LAGS = 64
ITERS = 2


def from_behind(value, axis, steps):
    count = lax.axis_size(axis)
    first, last = (max(0, -steps), min(count, count - steps))
    return lax.ppermute(value, axis, [(source, source + steps) for source in range(first, last)])


def xor_swap(value, axis, mask):
    count = lax.axis_size(axis)
    return lax.ppermute(value, axis, [(source, source ^ mask) for source in range(count)])


def masks_of(axis):
    count = lax.axis_size(axis)
    masks = []
    mask = 1
    while mask < count:
        masks.append(mask)
        mask *= 2
    return masks


def all_sum(value, axis):
    for mask in masks_of(axis):
        value = jax.tree.map(lambda a, b: a + b, value, xor_swap(value, axis, mask))
    return value


def ring_steps(axis):
    count = lax.axis_size(axis)
    if count != 8:
        return [
            ([source ^ mask for source in range(count)],
             [(source // mask) % 2 == 1 for source in range(count)])
            for mask in masks_of(axis)
        ]
    steps = [([source ^ 1 for source in range(8)], [source % 2 == 1 for source in range(8)])]
    for flip in (0, 1):
        partners, uppers = [], []
        for source in range(8):
            row, core = divmod(source, 2)
            if core == flip:
                other, upper = row ^ 1, row in (1, 2)
            else:
                other, upper = 3 - row, row in (2, 3)
            partners.append(2 * other + core)
            uppers.append(upper)
        steps.append((partners, uppers))
    return steps


def swap_with(value, axis, partners):
    return lax.ppermute(value, axis, [(source, target) for source, target in enumerate(partners)])


def upper_of(axis, uppers):
    return jnp.asarray(uppers)[lax.axis_index(axis)]


def sum_scatter(value, axis):
    for partners, uppers in ring_steps(axis):
        half = value.shape[0] // 2
        upper = upper_of(axis, uppers)
        send = lax.dynamic_slice_in_dim(value, jnp.where(upper, 0, half), half, axis=0)
        keep = lax.dynamic_slice_in_dim(value, jnp.where(upper, half, 0), half, axis=0)
        value = keep + swap_with(send, axis, partners)
    return value


def scatter_offset(axis, rows):
    offset = 0
    size = rows
    for partners, uppers in ring_steps(axis):
        size //= 2
        offset = offset + jnp.where(upper_of(axis, uppers), size, 0)
    return offset


def gather_rows(value, axis, dim=0):
    for partners, uppers in reversed(ring_steps(axis)):
        other = swap_with(value, axis, partners)
        upper = upper_of(axis, uppers)
        value = jnp.where(
            upper,
            jnp.concatenate([other, value], axis=dim),
            jnp.concatenate([value, other], axis=dim),
        )
    return value


def from_behind_other(value, steps):
    count = lax.axis_size("tm")
    pairs = [(2 * source + side, 2 * (source + steps) + 1 - side)
             for source in range(count - steps) for side in range(2)]
    return lax.ppermute(value, ("tm", "motif"), pairs)


CONV_DIMS = lax.ConvDimensionNumbers


def recon_of(weight_bfloat, hext):
    flipped = jnp.flip(weight_bfloat, axis=1)
    dims = CONV_DIMS((0, 1, 2), (2, 0, 1), (0, 1, 2))
    return lax.conv_general_dilated(
        hext[None], flipped, (1,), [(0, 0)], dimension_numbers=dims,
        preferred_element_type=jnp.float32,
    )[0]


def hnum_of(weight_bfloat, rext, chunk=16):
    k_dev, lags, n_dev = weight_bfloat.shape
    groups = lags // chunk
    width = rext.shape[1] - (lags - 1)
    grouped = weight_bfloat.reshape(k_dev * groups, chunk, n_dev)
    dims = CONV_DIMS((0, 1, 2), (0, 2, 1), (0, 1, 2))
    partial = lax.conv_general_dilated(
        rext[None], grouped, (1,), [(0, 0)], dimension_numbers=dims,
        preferred_element_type=jnp.float32,
    )[0].reshape(k_dev, groups, -1)
    total = partial[:, 0, :width]
    for group in range(1, groups):
        total = total + partial[:, group, chunk * group : chunk * group + width]
    return total


def wnum_of(hext, ratio, piece=32):
    k_dev, length = hext.shape
    n_dev, width = ratio.shape
    lags = length - width + 1
    pieces = width // piece
    spans = -(-(lags + piece) // piece)
    pad = (pieces + spans) * piece - length
    folded = jnp.pad(hext, ((0, 0), (0, pad))).reshape(k_dev, pieces + spans, piece)
    lhs = jnp.concatenate([folded[:, i : i + pieces, :] for i in range(spans)], axis=2)
    rhs = ratio.reshape(n_dev, pieces, piece)
    dims = CONV_DIMS((0, 1, 2), (0, 1, 2), (0, 2, 1))
    out = lax.conv_general_dilated(
        lhs, rhs, (1,), [(0, 0)], dimension_numbers=dims,
        preferred_element_type=jnp.float32,
    )
    return jnp.flip(out[:, :lags, :], axis=1)


def local(counts, motif_w, motif_h):
    k_dev, lags, n_dev = motif_w.shape
    width = counts.shape[1]
    rim = lags - 1
    rows = k_dev * lags
    scale_factor = 1.0 / (MOTIFS * LAGS)
    total_bins = width * lax.axis_size("tm")
    leading_bin = lax.axis_index("tm") * width
    spike_events = counts.astype(jnp.float32)
    weights = motif_w.reshape(rows, n_dev)
    weight_bfloat = motif_w.astype(jnp.bfloat16)
    half_k = k_dev // 2
    second = lax.axis_index("tm") % 2 == 1
    mine = jnp.where(second, weight_bfloat[half_k:], weight_bfloat[:half_k])
    fetched = xor_swap(mine, "motif", 1)
    relayed = xor_swap(fetched, "tm", 1)
    partner_w = jnp.where(
        second,
        jnp.concatenate([relayed, fetched], axis=0),
        jnp.concatenate([fetched, relayed], axis=0),
    )
    weight_all = jnp.concatenate([weight_bfloat, partner_w], axis=0)
    acts = motif_h
    offset = scatter_offset("tm", rows)
    part_rows = rows // lax.axis_size("tm")
    weight_part = lax.dynamic_slice_in_dim(weights, offset, part_rows, axis=0)
    place = jnp.arange(width + rim, dtype=jnp.int32)[:, None]
    lag_ids = jnp.arange(lags, dtype=jnp.int32)[None, :]
    window = ((place >= rim - lag_ids) & (place < rim - lag_ids + width)).astype(jnp.bfloat16)

    def extend_padded(acts):
        hbf = acts.astype(jnp.bfloat16)
        tail = hbf[:, width - rim :]
        own = jnp.concatenate([from_behind(tail, "tm", 1), hbf], axis=1)
        other = jnp.concatenate(
            [from_behind_other(tail, 1), xor_swap(hbf, "motif", 1)], axis=1
        )
        return own, jnp.concatenate([own, other], axis=0)

    def ratio_of(weight_all, hext_all):
        estimated_counts = recon_of(weight_all, hext_all) * scale_factor
        return (spike_events / estimated_counts).astype(jnp.bfloat16)

    bins = leading_bin + jnp.arange(width, dtype=jnp.int32)
    offsets = jnp.arange(lags, dtype=jnp.int32)
    mask = (bins[None, :] + offsets[:, None] < total_bins).astype(jnp.float32)
    hext, hext_all = extend_padded(acts)
    for step in range(ITERS):
        ratio = ratio_of(weight_all, hext_all)
        after = from_behind(ratio[:, :rim], "tm", -1)
        rext = jnp.concatenate([ratio, after], axis=1)
        hnum = hnum_of(weight_bfloat, rext)
        colsum = jnp.sum(weight_bfloat, axis=2, dtype=jnp.float32)
        joined = all_sum(jnp.concatenate([hnum, colsum], axis=1), "neuron")
        hnum, colsum = joined[:, :width], joined[:, width:]
        hden = jnp.dot(colsum, mask, precision=lax.Precision.HIGHEST)
        acts = acts * hnum / hden
        hext, hext_all = extend_padded(acts)
        ratio = ratio_of(weight_all, hext_all)
        wnum = wnum_of(hext, ratio).reshape(rows, n_dev)
        wden = jnp.dot(hext, window, preferred_element_type=jnp.float32).reshape(rows)
        blocks = lax.axis_size("tm")
        joined = jnp.concatenate(
            [wnum.reshape(blocks, part_rows, n_dev), wden.reshape(blocks, 1, part_rows)], axis=1
        )
        joined = sum_scatter(joined, "tm")[0]
        wnum, wden_part = joined[:part_rows], joined[part_rows]
        weight_part = weight_part * wnum / wden_part[:, None]
        if step + 1 < ITERS:
            part_bfloat = weight_part.astype(jnp.bfloat16)
            pair = jnp.stack([part_bfloat, xor_swap(part_bfloat, "motif", 1)], axis=0)
            pair = gather_rows(pair, "tm", dim=1)
            weight_all = pair.reshape(2 * k_dev, lags, n_dev)
            weight_bfloat = weight_all[:k_dev]
    weights = gather_rows(weight_part, "tm")
    return (weights.reshape(k_dev, lags, n_dev), acts)


def solution(mesh):
    in_specs = (P("neuron", "tm"), P("motif", None, "neuron"), P("motif", "tm"))
    out_specs = (P("motif", None, "neuron"), P("motif", "tm"))
    return jax.shard_map(local, mesh=mesh, in_specs=in_specs, out_specs=out_specs, check_vma=False)
```

```python
import jax
import jax.numpy as jnp
from jax import lax
from jax.sharding import PartitionSpec as P

MOTIFS = 64
LAGS = 64
ITERS = 2


def from_behind(value, axis, steps):
    count = lax.axis_size(axis)
    first, last = (max(0, -steps), min(count, count - steps))
    return lax.ppermute(value, axis, [(source, source + steps) for source in range(first, last)])


def xor_swap(value, axis, mask):
    count = lax.axis_size(axis)
    return lax.ppermute(value, axis, [(source, source ^ mask) for source in range(count)])


def masks_of(axis):
    count = lax.axis_size(axis)
    masks = []
    mask = 1
    while mask < count:
        masks.append(mask)
        mask *= 2
    return masks


def all_sum(value, axis):
    for mask in masks_of(axis):
        value = jax.tree.map(lambda a, b: a + b, value, xor_swap(value, axis, mask))
    return value


def ring_steps(axis):
    count = lax.axis_size(axis)
    if count != 8:
        return [
            ([source ^ mask for source in range(count)],
             [(source // mask) % 2 == 1 for source in range(count)])
            for mask in masks_of(axis)
        ]
    steps = [([source ^ 1 for source in range(8)], [source % 2 == 1 for source in range(8)])]
    for flip in (0, 1):
        partners, uppers = [], []
        for source in range(8):
            row, core = divmod(source, 2)
            if core == flip:
                other, upper = row ^ 1, row in (1, 2)
            else:
                other, upper = 3 - row, row in (2, 3)
            partners.append(2 * other + core)
            uppers.append(upper)
        steps.append((partners, uppers))
    return steps


def swap_with(value, axis, partners):
    return lax.ppermute(value, axis, [(source, target) for source, target in enumerate(partners)])


def upper_of(axis, uppers):
    return jnp.asarray(uppers)[lax.axis_index(axis)]


def sum_scatter(value, axis):
    for partners, uppers in ring_steps(axis):
        half = value.shape[0] // 2
        upper = upper_of(axis, uppers)
        send = lax.dynamic_slice_in_dim(value, jnp.where(upper, 0, half), half, axis=0)
        keep = lax.dynamic_slice_in_dim(value, jnp.where(upper, half, 0), half, axis=0)
        value = keep + swap_with(send, axis, partners)
    return value


def scatter_offset(axis, rows):
    offset = 0
    size = rows
    for partners, uppers in ring_steps(axis):
        size //= 2
        offset = offset + jnp.where(upper_of(axis, uppers), size, 0)
    return offset


def gather_rows(value, axis, dim=0):
    for partners, uppers in reversed(ring_steps(axis)):
        other = swap_with(value, axis, partners)
        upper = upper_of(axis, uppers)
        value = jnp.where(
            upper,
            jnp.concatenate([other, value], axis=dim),
            jnp.concatenate([value, other], axis=dim),
        )
    return value


def neuron_sum(value):
    count = lax.axis_size("neuron")
    rows = lax.axis_size("tm")
    if count != 8 or rows % 2:
        return all_sum(value, "neuron")
    value = value + xor_swap(value, "neuron", 1)
    for flip in (0, 1):
        pairs = []
        for row in range(rows):
            for source in range(count):
                ring, side = divmod(source, 2)
                other = ring ^ 1 if row % 2 == flip else 3 - ring
                pairs.append((row * count + source, row * count + 2 * other + side))
        value = value + lax.ppermute(value, ("tm", "neuron"), pairs)
    return value


def from_behind_other(value, steps):
    count = lax.axis_size("tm")
    pairs = [(2 * source + side, 2 * (source + steps) + 1 - side)
             for source in range(count - steps) for side in range(2)]
    return lax.ppermute(value, ("tm", "motif"), pairs)


CONV_DIMS = lax.ConvDimensionNumbers


def recon_of(weight_bfloat, hext):
    flipped = jnp.flip(weight_bfloat, axis=1)
    dims = CONV_DIMS((0, 1, 2), (2, 0, 1), (0, 1, 2))
    return lax.conv_general_dilated(
        hext[None], flipped, (1,), [(0, 0)], dimension_numbers=dims,
        preferred_element_type=jnp.float32,
    )[0]


def hnum_of(weight_bfloat, rext, chunk=16):
    k_dev, lags, n_dev = weight_bfloat.shape
    groups = lags // chunk
    width = rext.shape[1] - (lags - 1)
    grouped = weight_bfloat.reshape(k_dev * groups, chunk, n_dev)
    dims = CONV_DIMS((0, 1, 2), (0, 2, 1), (0, 1, 2))
    partial = lax.conv_general_dilated(
        rext[None], grouped, (1,), [(0, 0)], dimension_numbers=dims,
        preferred_element_type=jnp.float32,
    )[0].reshape(k_dev, groups, -1)
    total = partial[:, 0, :width]
    for group in range(1, groups):
        total = total + partial[:, group, chunk * group : chunk * group + width]
    return total


def wnum_of(hext, ratio, piece=32):
    k_dev, length = hext.shape
    n_dev, width = ratio.shape
    lags = length - width + 1
    pieces = width // piece
    spans = -(-(lags + piece) // piece)
    pad = (pieces + spans) * piece - length
    folded = jnp.pad(hext, ((0, 0), (0, pad))).reshape(k_dev, pieces + spans, piece)
    lhs = jnp.concatenate([folded[:, i : i + pieces, :] for i in range(spans)], axis=2)
    rhs = ratio.reshape(n_dev, pieces, piece)
    dims = CONV_DIMS((0, 1, 2), (0, 1, 2), (0, 2, 1))
    out = lax.conv_general_dilated(
        lhs, rhs, (1,), [(0, 0)], dimension_numbers=dims,
        preferred_element_type=jnp.float32,
    )
    return jnp.flip(out[:, :lags, :], axis=1)


def local(counts, motif_w, motif_h):
    k_dev, lags, n_dev = motif_w.shape
    width = counts.shape[1]
    rim = lags - 1
    rows = k_dev * lags
    scale_factor = 1.0 / (MOTIFS * LAGS)
    total_bins = width * lax.axis_size("tm")
    leading_bin = lax.axis_index("tm") * width
    spike_events = counts.astype(jnp.float32)
    weights = motif_w.reshape(rows, n_dev)
    weight_bfloat = motif_w.astype(jnp.bfloat16)
    half_k = k_dev // 2
    second = lax.axis_index("tm") % 2 == 1
    mine = jnp.where(second, weight_bfloat[half_k:], weight_bfloat[:half_k])
    fetched = xor_swap(mine, "motif", 1)
    relayed = xor_swap(fetched, "tm", 1)
    partner_w = jnp.where(
        second,
        jnp.concatenate([relayed, fetched], axis=0),
        jnp.concatenate([fetched, relayed], axis=0),
    )
    weight_all = jnp.concatenate([weight_bfloat, partner_w], axis=0)
    acts = motif_h
    offset = scatter_offset("tm", rows)
    part_rows = rows // lax.axis_size("tm")
    weight_part = lax.dynamic_slice_in_dim(weights, offset, part_rows, axis=0)
    place = jnp.arange(width + rim, dtype=jnp.int32)[:, None]
    lag_ids = jnp.arange(lags, dtype=jnp.int32)[None, :]
    window = ((place >= rim - lag_ids) & (place < rim - lag_ids + width)).astype(jnp.bfloat16)

    def extend_padded(acts):
        hbf = acts.astype(jnp.bfloat16)
        tail = hbf[:, width - rim :]
        own = jnp.concatenate([from_behind(tail, "tm", 1), hbf], axis=1)
        other = jnp.concatenate(
            [from_behind_other(tail, 1), xor_swap(hbf, "motif", 1)], axis=1
        )
        return own, jnp.concatenate([own, other], axis=0)

    def ratio_of(weight_all, hext_all):
        estimated_counts = recon_of(weight_all, hext_all) * scale_factor
        return (spike_events / estimated_counts).astype(jnp.bfloat16)

    bins = leading_bin + jnp.arange(width, dtype=jnp.int32)
    offsets = jnp.arange(lags, dtype=jnp.int32)
    mask = (bins[None, :] + offsets[:, None] < total_bins).astype(jnp.float32)
    hext, hext_all = extend_padded(acts)
    for step in range(ITERS):
        ratio = ratio_of(weight_all, hext_all)
        after = from_behind(ratio[:, :rim], "tm", -1)
        rext = jnp.concatenate([ratio, after], axis=1)
        hnum = hnum_of(weight_bfloat, rext)
        colsum = jnp.sum(weight_bfloat, axis=2, dtype=jnp.float32)
        joined = neuron_sum(jnp.concatenate([hnum, colsum], axis=1))
        hnum, colsum = joined[:, :width], joined[:, width:]
        hden = jnp.dot(colsum, mask, precision=lax.Precision.HIGHEST)
        acts = acts * hnum / hden
        hext, hext_all = extend_padded(acts)
        ratio = ratio_of(weight_all, hext_all)
        wnum = wnum_of(hext, ratio).reshape(rows, n_dev)
        wden = jnp.dot(hext, window, preferred_element_type=jnp.float32).reshape(rows)
        blocks = lax.axis_size("tm")
        joined = jnp.concatenate(
            [wnum.reshape(blocks, part_rows, n_dev), wden.reshape(blocks, 1, part_rows)], axis=1
        )
        joined = sum_scatter(joined, "tm")[0]
        wnum, wden_part = joined[:part_rows], joined[part_rows]
        weight_part = weight_part * wnum / wden_part[:, None]
        if step + 1 < ITERS:
            part_bfloat = weight_part.astype(jnp.bfloat16)
            pair = jnp.stack([part_bfloat, xor_swap(part_bfloat, "motif", 1)], axis=0)
            pair = gather_rows(pair, "tm", dim=1)
            weight_all = pair.reshape(2 * k_dev, lags, n_dev)
            weight_bfloat = weight_all[:k_dev]
    weights = gather_rows(weight_part, "tm")
    return (weights.reshape(k_dev, lags, n_dev), acts)


def solution(mesh):
    in_specs = (P("neuron", "tm"), P("motif", None, "neuron"), P("motif", "tm"))
    out_specs = (P("motif", None, "neuron"), P("motif", "tm"))
    return jax.shard_map(local, mesh=mesh, in_specs=in_specs, out_specs=out_specs, check_vma=False)
```

```python
import jax
import jax.numpy as jnp
from jax import lax
from jax.sharding import PartitionSpec as P

MOTIFS = 64
LAGS = 64
ITERS = 2


def from_behind(value, axis, steps):
    count = lax.axis_size(axis)
    first, last = (max(0, -steps), min(count, count - steps))
    return lax.ppermute(value, axis, [(source, source + steps) for source in range(first, last)])


def xor_swap(value, axis, mask):
    count = lax.axis_size(axis)
    return lax.ppermute(value, axis, [(source, source ^ mask) for source in range(count)])


def masks_of(axis):
    count = lax.axis_size(axis)
    masks = []
    mask = 1
    while mask < count:
        masks.append(mask)
        mask *= 2
    return masks


def all_sum(value, axis):
    for mask in masks_of(axis):
        value = jax.tree.map(lambda a, b: a + b, value, xor_swap(value, axis, mask))
    return value


def ring_steps(axis):
    count = lax.axis_size(axis)
    if count != 8:
        return [
            ([source ^ mask for source in range(count)],
             [(source // mask) % 2 == 1 for source in range(count)])
            for mask in masks_of(axis)
        ]
    steps = [([source ^ 1 for source in range(8)], [source % 2 == 1 for source in range(8)])]
    for flip in (0, 1):
        partners, uppers = [], []
        for source in range(8):
            row, core = divmod(source, 2)
            if core == flip:
                other, upper = row ^ 1, row in (1, 2)
            else:
                other, upper = 3 - row, row in (2, 3)
            partners.append(2 * other + core)
            uppers.append(upper)
        steps.append((partners, uppers))
    return steps


def swap_with(value, axis, partners):
    return lax.ppermute(value, axis, [(source, target) for source, target in enumerate(partners)])


def upper_of(axis, uppers):
    return jnp.asarray(uppers)[lax.axis_index(axis)]


def sum_scatter(value, axis):
    for partners, uppers in ring_steps(axis):
        half = value.shape[0] // 2
        upper = upper_of(axis, uppers)
        send = lax.dynamic_slice_in_dim(value, jnp.where(upper, 0, half), half, axis=0)
        keep = lax.dynamic_slice_in_dim(value, jnp.where(upper, half, 0), half, axis=0)
        value = keep + swap_with(send, axis, partners)
    return value


def scatter_offset(axis, rows):
    offset = 0
    size = rows
    for partners, uppers in ring_steps(axis):
        size //= 2
        offset = offset + jnp.where(upper_of(axis, uppers), size, 0)
    return offset


def gather_rows(value, axis, dim=0):
    for partners, uppers in reversed(ring_steps(axis)):
        other = swap_with(value, axis, partners)
        upper = upper_of(axis, uppers)
        value = jnp.where(
            upper,
            jnp.concatenate([other, value], axis=dim),
            jnp.concatenate([value, other], axis=dim),
        )
    return value


def neuron_sum(value):
    count = lax.axis_size("neuron")
    rows = lax.axis_size("tm")
    if count != 8 or rows % 2:
        return all_sum(value, "neuron")
    value = value + xor_swap(value, "neuron", 1)
    for flip in (0, 1):
        pairs = []
        for row in range(rows):
            for source in range(count):
                ring, side = divmod(source, 2)
                other = ring ^ 1 if row % 2 == flip else 3 - ring
                pairs.append((row * count + source, row * count + 2 * other + side))
        value = value + lax.ppermute(value, ("tm", "neuron"), pairs)
    return value


def from_behind_other(value, steps):
    count = lax.axis_size("tm")
    pairs = [(2 * source + side, 2 * (source + steps) + 1 - side)
             for source in range(count - steps) for side in range(2)]
    return lax.ppermute(value, ("tm", "motif"), pairs)


CONV_DIMS = lax.ConvDimensionNumbers


def recon_of(weight_bfloat, hext):
    flipped = jnp.flip(weight_bfloat, axis=1)
    dims = CONV_DIMS((0, 1, 2), (2, 0, 1), (0, 1, 2))
    return lax.conv_general_dilated(
        hext[None], flipped, (1,), [(0, 0)], dimension_numbers=dims,
        preferred_element_type=jnp.float32,
    )[0]


def hnum_of(weight_bfloat, rext, chunk=16):
    k_dev, lags, n_dev = weight_bfloat.shape
    groups = lags // chunk
    width = rext.shape[1] - (lags - 1)
    grouped = weight_bfloat.reshape(k_dev * groups, chunk, n_dev)
    dims = CONV_DIMS((0, 1, 2), (0, 2, 1), (0, 1, 2))
    partial = lax.conv_general_dilated(
        rext[None], grouped, (1,), [(0, 0)], dimension_numbers=dims,
        preferred_element_type=jnp.float32,
    )[0].reshape(k_dev, groups, -1)
    total = partial[:, 0, :width]
    for group in range(1, groups):
        total = total + partial[:, group, chunk * group : chunk * group + width]
    return total


def wnum_of(hext, ratio, piece=32):
    k_dev, length = hext.shape
    n_dev, width = ratio.shape
    lags = length - width + 1
    pieces = width // piece
    spans = -(-(lags + piece) // piece)
    pad = (pieces + spans) * piece - length
    folded = jnp.pad(hext, ((0, 0), (0, pad))).reshape(k_dev, pieces + spans, piece)
    lhs = jnp.concatenate([folded[:, i : i + pieces, :] for i in range(spans)], axis=2)
    rhs = ratio.reshape(n_dev, pieces, piece)
    dims = CONV_DIMS((0, 1, 2), (0, 1, 2), (0, 2, 1))
    out = lax.conv_general_dilated(
        lhs, rhs, (1,), [(0, 0)], dimension_numbers=dims,
        preferred_element_type=jnp.float32,
    )
    return out[:, :lags, :]


def local(counts, motif_w, motif_h):
    k_dev, lags, n_dev = motif_w.shape
    width = counts.shape[1]
    rim = lags - 1
    rows = k_dev * lags
    scale_factor = 1.0 / (MOTIFS * LAGS)
    total_bins = width * lax.axis_size("tm")
    leading_bin = lax.axis_index("tm") * width
    spike_events = counts.astype(jnp.float32)
    weights = motif_w.reshape(rows, n_dev)
    weight_bfloat = motif_w.astype(jnp.bfloat16)
    half_k = k_dev // 2
    second = lax.axis_index("tm") % 2 == 1
    mine = jnp.where(second, weight_bfloat[half_k:], weight_bfloat[:half_k])
    fetched = xor_swap(mine, "motif", 1)
    relayed = xor_swap(fetched, "tm", 1)
    partner_w = jnp.where(
        second,
        jnp.concatenate([relayed, fetched], axis=0),
        jnp.concatenate([fetched, relayed], axis=0),
    )
    weight_all = jnp.concatenate([weight_bfloat, partner_w], axis=0)
    acts = motif_h
    offset = scatter_offset("tm", rows)
    part_rows = rows // lax.axis_size("tm")
    def flip_lags(part):
        return jnp.flip(part.reshape(-1, lags, n_dev), axis=1).reshape(part.shape)

    weight_part = flip_lags(lax.dynamic_slice_in_dim(weights, offset, part_rows, axis=0))
    place = jnp.arange(width + rim, dtype=jnp.int32)[:, None]
    lag_ids = jnp.arange(lags, dtype=jnp.int32)[None, :]
    window = ((place >= lag_ids) & (place < lag_ids + width)).astype(jnp.bfloat16)

    def extend_padded(acts):
        hbf = acts.astype(jnp.bfloat16)
        tail = hbf[:, width - rim :]
        own = jnp.concatenate([from_behind(tail, "tm", 1), hbf], axis=1)
        other = jnp.concatenate(
            [from_behind_other(tail, 1), xor_swap(hbf, "motif", 1)], axis=1
        )
        return own, jnp.concatenate([own, other], axis=0)

    def ratio_of(weight_all, hext_all):
        estimated_counts = recon_of(weight_all, hext_all) * scale_factor
        return (spike_events / estimated_counts).astype(jnp.bfloat16)

    bins = leading_bin + jnp.arange(width, dtype=jnp.int32)
    offsets = jnp.arange(lags, dtype=jnp.int32)
    mask = (bins[None, :] + offsets[:, None] < total_bins).astype(jnp.float32)
    hext, hext_all = extend_padded(acts)
    for step in range(ITERS):
        ratio = ratio_of(weight_all, hext_all)
        after = from_behind(ratio[:, :rim], "tm", -1)
        rext = jnp.concatenate([ratio, after], axis=1)
        hnum = hnum_of(weight_bfloat, rext)
        colsum = jnp.sum(weight_bfloat, axis=2, dtype=jnp.float32)
        joined = neuron_sum(jnp.concatenate([hnum, colsum], axis=1))
        hnum, colsum = joined[:, :width], joined[:, width:]
        hden = jnp.dot(colsum, mask, precision=lax.Precision.HIGHEST)
        acts = acts * hnum / hden
        hext, hext_all = extend_padded(acts)
        ratio = ratio_of(weight_all, hext_all)
        wnum = wnum_of(hext, ratio).reshape(rows, n_dev)
        wden = jnp.dot(hext, window, preferred_element_type=jnp.float32).reshape(rows)
        blocks = lax.axis_size("tm")
        joined = jnp.concatenate(
            [wnum.reshape(blocks, part_rows, n_dev), wden.reshape(blocks, 1, part_rows)], axis=1
        )
        joined = sum_scatter(joined, "tm")[0]
        wnum, wden_part = joined[:part_rows], joined[part_rows]
        weight_part = weight_part * wnum / wden_part[:, None]
        if step + 1 < ITERS:
            part_bfloat = flip_lags(weight_part).astype(jnp.bfloat16)
            pair = jnp.stack([part_bfloat, xor_swap(part_bfloat, "motif", 1)], axis=0)
            pair = gather_rows(pair, "tm", dim=1)
            weight_all = pair.reshape(2 * k_dev, lags, n_dev)
            weight_bfloat = weight_all[:k_dev]
    weights = gather_rows(flip_lags(weight_part), "tm")
    return (weights.reshape(k_dev, lags, n_dev), acts)


def solution(mesh):
    in_specs = (P("neuron", "tm"), P("motif", None, "neuron"), P("motif", "tm"))
    out_specs = (P("motif", None, "neuron"), P("motif", "tm"))
    return jax.shard_map(local, mesh=mesh, in_specs=in_specs, out_specs=out_specs, check_vma=False)
```

```python
import jax
import jax.numpy as jnp
from jax import lax
from jax.sharding import PartitionSpec as P

MOTIFS = 64
LAGS = 64
ITERS = 2


def from_behind(value, axis, steps):
    count = lax.axis_size(axis)
    first, last = (max(0, -steps), min(count, count - steps))
    return lax.ppermute(value, axis, [(source, source + steps) for source in range(first, last)])


def xor_swap(value, axis, mask):
    count = lax.axis_size(axis)
    return lax.ppermute(value, axis, [(source, source ^ mask) for source in range(count)])


def masks_of(axis):
    count = lax.axis_size(axis)
    masks = []
    mask = 1
    while mask < count:
        masks.append(mask)
        mask *= 2
    return masks


def all_sum(value, axis):
    for mask in masks_of(axis):
        value = jax.tree.map(lambda a, b: a + b, value, xor_swap(value, axis, mask))
    return value


def ring_steps(axis):
    count = lax.axis_size(axis)
    if count != 8:
        return [
            ([source ^ mask for source in range(count)],
             [(source // mask) % 2 == 1 for source in range(count)])
            for mask in masks_of(axis)
        ]
    steps = [([source ^ 1 for source in range(8)], [source % 2 == 1 for source in range(8)])]
    for flip in (0, 1):
        partners, uppers = [], []
        for source in range(8):
            row, core = divmod(source, 2)
            if core == flip:
                other, upper = row ^ 1, row in (1, 2)
            else:
                other, upper = 3 - row, row in (2, 3)
            partners.append(2 * other + core)
            uppers.append(upper)
        steps.append((partners, uppers))
    return steps


def swap_with(value, axis, partners):
    return lax.ppermute(value, axis, [(source, target) for source, target in enumerate(partners)])


def upper_of(axis, uppers):
    return jnp.asarray(uppers)[lax.axis_index(axis)]


def sum_scatter(value, axis):
    for partners, uppers in ring_steps(axis):
        half = value.shape[0] // 2
        upper = upper_of(axis, uppers)
        send = lax.dynamic_slice_in_dim(value, jnp.where(upper, 0, half), half, axis=0)
        keep = lax.dynamic_slice_in_dim(value, jnp.where(upper, half, 0), half, axis=0)
        value = keep + swap_with(send, axis, partners)
    return value


def scatter_offset(axis, rows):
    offset = 0
    size = rows
    for partners, uppers in ring_steps(axis):
        size //= 2
        offset = offset + jnp.where(upper_of(axis, uppers), size, 0)
    return offset


def gather_rows(value, axis, dim=0):
    for partners, uppers in reversed(ring_steps(axis)):
        other = swap_with(value, axis, partners)
        upper = upper_of(axis, uppers)
        value = jnp.where(
            upper,
            jnp.concatenate([other, value], axis=dim),
            jnp.concatenate([value, other], axis=dim),
        )
    return value


def neuron_sum(value):
    count = lax.axis_size("neuron")
    rows = lax.axis_size("tm")
    if count != 8 or rows % 2:
        return all_sum(value, "neuron")
    value = value + xor_swap(value, "neuron", 1)
    for flip in (0, 1):
        pairs = []
        for row in range(rows):
            for source in range(count):
                ring, side = divmod(source, 2)
                other = ring ^ 1 if row % 2 == flip else 3 - ring
                pairs.append((row * count + source, row * count + 2 * other + side))
        value = value + lax.ppermute(value, ("tm", "neuron"), pairs)
    return value


def from_behind_other(value, steps):
    count = lax.axis_size("tm")
    pairs = [(2 * source + side, 2 * (source + steps) + 1 - side)
             for source in range(count - steps) for side in range(2)]
    return lax.ppermute(value, ("tm", "motif"), pairs)


CONV_DIMS = lax.ConvDimensionNumbers


def recon_of(weight_bfloat, hext):
    flipped = jnp.flip(weight_bfloat, axis=1)
    dims = CONV_DIMS((0, 1, 2), (2, 0, 1), (0, 1, 2))
    return lax.conv_general_dilated(
        hext[None], flipped, (1,), [(0, 0)], dimension_numbers=dims,
        preferred_element_type=jnp.float32,
    )[0]


def hnum_of(weight_bfloat, rext, chunk=32):
    k_dev, lags, n_dev = weight_bfloat.shape
    groups = lags // chunk
    width = rext.shape[1] - (lags - 1)
    grouped = weight_bfloat.reshape(k_dev * groups, chunk, n_dev)
    dims = CONV_DIMS((0, 1, 2), (0, 2, 1), (0, 1, 2))
    partial = lax.conv_general_dilated(
        rext[None], grouped, (1,), [(0, 0)], dimension_numbers=dims,
        preferred_element_type=jnp.float32,
    )[0].reshape(k_dev, groups, -1)
    total = partial[:, 0, :width]
    for group in range(1, groups):
        total = total + partial[:, group, chunk * group : chunk * group + width]
    return total


def wnum_of(hext, ratio, piece=32):
    k_dev, length = hext.shape
    n_dev, width = ratio.shape
    lags = length - width + 1
    pieces = width // piece
    spans = -(-(lags + piece) // piece)
    pad = (pieces + spans) * piece - length
    folded = jnp.pad(hext, ((0, 0), (0, pad))).reshape(k_dev, pieces + spans, piece)
    lhs = jnp.concatenate([folded[:, i : i + pieces, :] for i in range(spans)], axis=2)
    rhs = ratio.reshape(n_dev, pieces, piece)
    dims = CONV_DIMS((0, 1, 2), (0, 1, 2), (0, 2, 1))
    out = lax.conv_general_dilated(
        lhs, rhs, (1,), [(0, 0)], dimension_numbers=dims,
        preferred_element_type=jnp.float32,
    )
    return out[:, :lags, :]


def local(counts, motif_w, motif_h):
    k_dev, lags, n_dev = motif_w.shape
    width = counts.shape[1]
    rim = lags - 1
    rows = k_dev * lags
    scale_factor = 1.0 / (MOTIFS * LAGS)
    total_bins = width * lax.axis_size("tm")
    leading_bin = lax.axis_index("tm") * width
    spike_events = counts.astype(jnp.float32)
    weights = motif_w.reshape(rows, n_dev)
    weight_bfloat = motif_w.astype(jnp.bfloat16)
    half_k = k_dev // 2
    second = lax.axis_index("tm") % 2 == 1
    mine = jnp.where(second, weight_bfloat[half_k:], weight_bfloat[:half_k])
    fetched = xor_swap(mine, "motif", 1)
    relayed = xor_swap(fetched, "tm", 1)
    partner_w = jnp.where(
        second,
        jnp.concatenate([relayed, fetched], axis=0),
        jnp.concatenate([fetched, relayed], axis=0),
    )
    weight_all = jnp.concatenate([weight_bfloat, partner_w], axis=0)
    acts = motif_h
    offset = scatter_offset("tm", rows)
    part_rows = rows // lax.axis_size("tm")
    def flip_lags(part):
        return jnp.flip(part.reshape(-1, lags, n_dev), axis=1).reshape(part.shape)

    weight_part = flip_lags(lax.dynamic_slice_in_dim(weights, offset, part_rows, axis=0))
    place = jnp.arange(width + rim, dtype=jnp.int32)[:, None]
    lag_ids = jnp.arange(lags, dtype=jnp.int32)[None, :]
    window = ((place >= lag_ids) & (place < lag_ids + width)).astype(jnp.bfloat16)

    def extend_padded(acts):
        hbf = acts.astype(jnp.bfloat16)
        tail = hbf[:, width - rim :]
        own = jnp.concatenate([from_behind(tail, "tm", 1), hbf], axis=1)
        other = jnp.concatenate(
            [from_behind_other(tail, 1), xor_swap(hbf, "motif", 1)], axis=1
        )
        return own, jnp.concatenate([own, other], axis=0)

    def ratio_of(weight_all, hext_all):
        estimated_counts = recon_of(weight_all, hext_all) * scale_factor
        return (spike_events / estimated_counts).astype(jnp.bfloat16)

    bins = leading_bin + jnp.arange(width, dtype=jnp.int32)
    offsets = jnp.arange(lags, dtype=jnp.int32)
    mask = (bins[None, :] + offsets[:, None] < total_bins).astype(jnp.float32)
    hext, hext_all = extend_padded(acts)
    for step in range(ITERS):
        ratio = ratio_of(weight_all, hext_all)
        after = from_behind(ratio[:, :rim], "tm", -1)
        rext = jnp.concatenate([ratio, after], axis=1)
        hnum = hnum_of(weight_bfloat, rext)
        colsum = jnp.sum(weight_bfloat, axis=2, dtype=jnp.float32)
        joined = neuron_sum(jnp.concatenate([hnum, colsum], axis=1))
        hnum, colsum = joined[:, :width], joined[:, width:]
        hden = jnp.dot(colsum, mask, precision=lax.Precision.HIGHEST)
        acts = acts * hnum / hden
        hext, hext_all = extend_padded(acts)
        ratio = ratio_of(weight_all, hext_all)
        wnum = wnum_of(hext, ratio).reshape(rows, n_dev)
        wden = jnp.dot(hext, window, preferred_element_type=jnp.float32).reshape(rows)
        blocks = lax.axis_size("tm")
        joined = jnp.concatenate(
            [wnum.reshape(blocks, part_rows, n_dev), wden.reshape(blocks, 1, part_rows)], axis=1
        )
        joined = sum_scatter(joined, "tm")[0]
        wnum, wden_part = joined[:part_rows], joined[part_rows]
        weight_part = weight_part * wnum / wden_part[:, None]
        if step + 1 < ITERS:
            part_bfloat = flip_lags(weight_part).astype(jnp.bfloat16)
            pair = jnp.stack([part_bfloat, xor_swap(part_bfloat, "motif", 1)], axis=0)
            pair = gather_rows(pair, "tm", dim=1)
            weight_all = pair.reshape(2 * k_dev, lags, n_dev)
            weight_bfloat = weight_all[:k_dev]
    weights = gather_rows(flip_lags(weight_part), "tm")
    return (weights.reshape(k_dev, lags, n_dev), acts)


def solution(mesh):
    in_specs = (P("neuron", "tm"), P("motif", None, "neuron"), P("motif", "tm"))
    out_specs = (P("motif", None, "neuron"), P("motif", "tm"))
    return jax.shard_map(local, mesh=mesh, in_specs=in_specs, out_specs=out_specs, check_vma=False)
```

```python
import jax
import jax.numpy as jnp
from jax import lax
from jax.sharding import PartitionSpec as P

MOTIFS = 64
LAGS = 64
ITERS = 2


def from_behind(value, axis, steps):
    count = lax.axis_size(axis)
    first, last = (max(0, -steps), min(count, count - steps))
    return lax.ppermute(value, axis, [(source, source + steps) for source in range(first, last)])


def xor_swap(value, axis, mask):
    count = lax.axis_size(axis)
    return lax.ppermute(value, axis, [(source, source ^ mask) for source in range(count)])


def masks_of(axis):
    count = lax.axis_size(axis)
    masks = []
    mask = 1
    while mask < count:
        masks.append(mask)
        mask *= 2
    return masks


def all_sum(value, axis):
    for mask in masks_of(axis):
        value = jax.tree.map(lambda a, b: a + b, value, xor_swap(value, axis, mask))
    return value


def ring_steps(axis):
    count = lax.axis_size(axis)
    if count != 8:
        return [
            ([source ^ mask for source in range(count)],
             [(source // mask) % 2 == 1 for source in range(count)])
            for mask in masks_of(axis)
        ]
    steps = [([source ^ 1 for source in range(8)], [source % 2 == 1 for source in range(8)])]
    for flip in (0, 1):
        partners, uppers = [], []
        for source in range(8):
            row, core = divmod(source, 2)
            if core == flip:
                other, upper = row ^ 1, row in (1, 2)
            else:
                other, upper = 3 - row, row in (2, 3)
            partners.append(2 * other + core)
            uppers.append(upper)
        steps.append((partners, uppers))
    return steps


def swap_with(value, axis, partners):
    return lax.ppermute(value, axis, [(source, target) for source, target in enumerate(partners)])


def upper_of(axis, uppers):
    return jnp.asarray(uppers)[lax.axis_index(axis)]


def sum_scatter(value, axis):
    for partners, uppers in ring_steps(axis):
        half = value.shape[0] // 2
        upper = upper_of(axis, uppers)
        send = lax.dynamic_slice_in_dim(value, jnp.where(upper, 0, half), half, axis=0)
        keep = lax.dynamic_slice_in_dim(value, jnp.where(upper, half, 0), half, axis=0)
        value = keep + swap_with(send, axis, partners)
    return value


def scatter_offset(axis, rows):
    offset = 0
    size = rows
    for partners, uppers in ring_steps(axis):
        size //= 2
        offset = offset + jnp.where(upper_of(axis, uppers), size, 0)
    return offset


def gather_rows(value, axis, dim=0):
    for partners, uppers in reversed(ring_steps(axis)):
        other = swap_with(value, axis, partners)
        upper = upper_of(axis, uppers)
        value = jnp.where(
            upper,
            jnp.concatenate([other, value], axis=dim),
            jnp.concatenate([value, other], axis=dim),
        )
    return value


def neuron_sum(value):
    count = lax.axis_size("neuron")
    rows = lax.axis_size("tm")
    if count != 8 or rows % 2:
        return all_sum(value, "neuron")
    value = value + xor_swap(value, "neuron", 1)
    for flip in (0, 1):
        pairs = []
        for row in range(rows):
            for source in range(count):
                ring, side = divmod(source, 2)
                other = ring ^ 1 if row % 2 == flip else 3 - ring
                pairs.append((row * count + source, row * count + 2 * other + side))
        value = value + lax.ppermute(value, ("tm", "neuron"), pairs)
    return value


def from_behind_other(value, steps):
    count = lax.axis_size("tm")
    pairs = [(2 * source + side, 2 * (source + steps) + 1 - side)
             for source in range(count - steps) for side in range(2)]
    return lax.ppermute(value, ("tm", "motif"), pairs)


CONV_DIMS = lax.ConvDimensionNumbers


def recon_of(weight_bfloat, hext):
    flipped = jnp.flip(weight_bfloat, axis=1)
    dims = CONV_DIMS((0, 1, 2), (2, 0, 1), (0, 1, 2))
    return lax.conv_general_dilated(
        hext[None], flipped, (1,), [(0, 0)], dimension_numbers=dims,
        preferred_element_type=jnp.float32,
    )[0]


def hnum_of(weight_bfloat, rext, chunk=16):
    k_dev, lags, n_dev = weight_bfloat.shape
    groups = lags // chunk
    width = rext.shape[1] - (lags - 1)
    grouped = weight_bfloat.reshape(k_dev * groups, chunk, n_dev)
    dims = CONV_DIMS((0, 1, 2), (0, 2, 1), (0, 1, 2))
    partial = lax.conv_general_dilated(
        rext[None], grouped, (1,), [(0, 0)], dimension_numbers=dims,
        preferred_element_type=jnp.float32,
    )[0].reshape(k_dev, groups, -1)
    total = partial[:, 0, :width]
    for group in range(1, groups):
        total = total + partial[:, group, chunk * group : chunk * group + width]
    return total


def wnum_of(hext, ratio, piece=32):
    k_dev, length = hext.shape
    n_dev, width = ratio.shape
    lags = length - width + 1
    pieces = width // piece
    spans = -(-(lags + piece) // piece)
    pad = (pieces + spans) * piece - length
    folded = jnp.pad(hext, ((0, 0), (0, pad))).reshape(k_dev, pieces + spans, piece)
    lhs = jnp.concatenate([folded[:, i : i + pieces, :] for i in range(spans)], axis=2)
    rhs = ratio.reshape(n_dev, pieces, piece)
    dims = CONV_DIMS((0, 1, 2), (0, 1, 2), (0, 2, 1))
    out = lax.conv_general_dilated(
        lhs, rhs, (1,), [(0, 0)], dimension_numbers=dims,
        preferred_element_type=jnp.float32,
    )
    return out[:, :lags, :]


def local(counts, motif_w, motif_h):
    k_dev, lags, n_dev = motif_w.shape
    width = counts.shape[1]
    rim = lags - 1
    rows = k_dev * lags
    scale_factor = 1.0 / (MOTIFS * LAGS)
    total_bins = width * lax.axis_size("tm")
    leading_bin = lax.axis_index("tm") * width
    spike_events = counts.astype(jnp.float32)
    weights = motif_w.reshape(rows, n_dev)
    weight_bfloat = motif_w.astype(jnp.bfloat16)
    half_k = k_dev // 2
    second = lax.axis_index("tm") % 2 == 1
    mine = jnp.where(second, weight_bfloat[half_k:], weight_bfloat[:half_k])
    fetched = xor_swap(mine, "motif", 1)
    relayed = xor_swap(fetched, "tm", 1)
    partner_w = jnp.where(
        second,
        jnp.concatenate([relayed, fetched], axis=0),
        jnp.concatenate([fetched, relayed], axis=0),
    )
    weight_all = jnp.concatenate([weight_bfloat, partner_w], axis=0)
    acts = motif_h
    offset = scatter_offset("tm", rows)
    part_rows = rows // lax.axis_size("tm")
    def flip_lags(part):
        return jnp.flip(part.reshape(-1, lags, n_dev), axis=1).reshape(part.shape)

    weight_part = flip_lags(lax.dynamic_slice_in_dim(weights, offset, part_rows, axis=0))
    place = jnp.arange(width + rim, dtype=jnp.int32)[:, None]
    lag_ids = jnp.arange(lags, dtype=jnp.int32)[None, :]
    window = ((place >= lag_ids) & (place < lag_ids + width)).astype(jnp.bfloat16)

    def extend_padded(acts):
        hbf = acts.astype(jnp.bfloat16)
        tail = hbf[:, width - rim :]
        own = jnp.concatenate([from_behind(tail, "tm", 1), hbf], axis=1)
        other = jnp.concatenate(
            [from_behind_other(tail, 1), xor_swap(hbf, "motif", 1)], axis=1
        )
        return own, jnp.concatenate([own, other], axis=0)

    def ratio_of(weight_all, hext_all):
        estimated_counts = recon_of(weight_all, hext_all) * scale_factor
        return (spike_events / estimated_counts).astype(jnp.bfloat16)

    bins = leading_bin + jnp.arange(width, dtype=jnp.int32)
    offsets = jnp.arange(lags, dtype=jnp.int32)
    mask = (bins[None, :] + offsets[:, None] < total_bins).astype(jnp.float32)
    hext, hext_all = extend_padded(acts)
    for step in range(ITERS):
        ratio = ratio_of(weight_all, hext_all)
        after = from_behind(ratio[:, :rim], "tm", -1)
        inner = hnum_of(weight_bfloat, ratio)
        edge = hnum_of(weight_bfloat, jnp.concatenate([ratio[:, width - rim :], after], axis=1))
        hnum = jnp.concatenate([inner, edge], axis=1)
        colsum = jnp.sum(weight_bfloat, axis=2, dtype=jnp.float32)
        joined = neuron_sum(jnp.concatenate([hnum, colsum], axis=1))
        hnum, colsum = joined[:, :width], joined[:, width:]
        hden = jnp.dot(colsum, mask, precision=lax.Precision.HIGHEST)
        acts = acts * hnum / hden
        hext, hext_all = extend_padded(acts)
        ratio = ratio_of(weight_all, hext_all)
        wnum = wnum_of(hext, ratio).reshape(rows, n_dev)
        wden = jnp.dot(hext, window, preferred_element_type=jnp.float32).reshape(rows)
        blocks = lax.axis_size("tm")
        joined = jnp.concatenate(
            [wnum.reshape(blocks, part_rows, n_dev), wden.reshape(blocks, 1, part_rows)], axis=1
        )
        joined = sum_scatter(joined, "tm")[0]
        wnum, wden_part = joined[:part_rows], joined[part_rows]
        weight_part = weight_part * wnum / wden_part[:, None]
        if step + 1 < ITERS:
            part_bfloat = flip_lags(weight_part).astype(jnp.bfloat16)
            pair = jnp.stack([part_bfloat, xor_swap(part_bfloat, "motif", 1)], axis=0)
            pair = gather_rows(pair, "tm", dim=1)
            weight_all = pair.reshape(2 * k_dev, lags, n_dev)
            weight_bfloat = weight_all[:k_dev]
    weights = gather_rows(flip_lags(weight_part), "tm")
    return (weights.reshape(k_dev, lags, n_dev), acts)


def solution(mesh):
    in_specs = (P("neuron", "tm"), P("motif", None, "neuron"), P("motif", "tm"))
    out_specs = (P("motif", None, "neuron"), P("motif", "tm"))
    return jax.shard_map(local, mesh=mesh, in_specs=in_specs, out_specs=out_specs, check_vma=False)
```

```python
import jax
import jax.numpy as jnp
from jax import lax
from jax.sharding import PartitionSpec as P

MOTIFS = 64
LAGS = 64
ITERS = 2


def from_behind(value, axis, steps):
    count = lax.axis_size(axis)
    first, last = (max(0, -steps), min(count, count - steps))
    return lax.ppermute(value, axis, [(source, source + steps) for source in range(first, last)])


def xor_swap(value, axis, mask):
    count = lax.axis_size(axis)
    return lax.ppermute(value, axis, [(source, source ^ mask) for source in range(count)])


def masks_of(axis):
    count = lax.axis_size(axis)
    masks = []
    mask = 1
    while mask < count:
        masks.append(mask)
        mask *= 2
    return masks


def all_sum(value, axis):
    for mask in masks_of(axis):
        value = jax.tree.map(lambda a, b: a + b, value, xor_swap(value, axis, mask))
    return value


def ring_steps(axis):
    count = lax.axis_size(axis)
    if count != 8:
        return [
            ([source ^ mask for source in range(count)],
             [(source // mask) % 2 == 1 for source in range(count)])
            for mask in masks_of(axis)
        ]
    steps = [([source ^ 1 for source in range(8)], [source % 2 == 1 for source in range(8)])]
    for flip in (0, 1):
        partners, uppers = [], []
        for source in range(8):
            row, core = divmod(source, 2)
            if core == flip:
                other, upper = row ^ 1, row in (1, 2)
            else:
                other, upper = 3 - row, row in (2, 3)
            partners.append(2 * other + core)
            uppers.append(upper)
        steps.append((partners, uppers))
    return steps


def swap_with(value, axis, partners):
    return lax.ppermute(value, axis, [(source, target) for source, target in enumerate(partners)])


def upper_of(axis, uppers):
    return jnp.asarray(uppers)[lax.axis_index(axis)]


def sum_scatter(value, axis):
    for partners, uppers in ring_steps(axis):
        half = value.shape[0] // 2
        upper = upper_of(axis, uppers)
        send = lax.dynamic_slice_in_dim(value, jnp.where(upper, 0, half), half, axis=0)
        keep = lax.dynamic_slice_in_dim(value, jnp.where(upper, half, 0), half, axis=0)
        value = keep + swap_with(send, axis, partners)
    return value


def scatter_offset(axis, rows):
    offset = 0
    size = rows
    for partners, uppers in ring_steps(axis):
        size //= 2
        offset = offset + jnp.where(upper_of(axis, uppers), size, 0)
    return offset


def gather_rows(value, axis, dim=0):
    for partners, uppers in reversed(ring_steps(axis)):
        other = swap_with(value, axis, partners)
        upper = upper_of(axis, uppers)
        value = jnp.where(
            upper,
            jnp.concatenate([other, value], axis=dim),
            jnp.concatenate([value, other], axis=dim),
        )
    return value


def neuron_sum(value):
    count = lax.axis_size("neuron")
    rows = lax.axis_size("tm")
    if count != 8 or rows % 2:
        return all_sum(value, "neuron")
    value = value + xor_swap(value, "neuron", 1)
    for flip in (0, 1):
        pairs = []
        for row in range(rows):
            for source in range(count):
                ring, side = divmod(source, 2)
                other = ring ^ 1 if row % 2 == flip else 3 - ring
                pairs.append((row * count + source, row * count + 2 * other + side))
        value = value + lax.ppermute(value, ("tm", "neuron"), pairs)
    return value


def from_behind_other(value, steps):
    count = lax.axis_size("tm")
    pairs = [(2 * source + side, 2 * (source + steps) + 1 - side)
             for source in range(count - steps) for side in range(2)]
    return lax.ppermute(value, ("tm", "motif"), pairs)


CONV_DIMS = lax.ConvDimensionNumbers


def recon_of(weight_bfloat, hext):
    flipped = jnp.flip(weight_bfloat, axis=1)
    dims = CONV_DIMS((0, 1, 2), (2, 0, 1), (0, 1, 2))
    return lax.conv_general_dilated(
        hext[None], flipped, (1,), [(0, 0)], dimension_numbers=dims,
        preferred_element_type=jnp.float32,
    )[0]


def hnum_of(weight_bfloat, rext, chunk=16):
    k_dev, lags, n_dev = weight_bfloat.shape
    groups = lags // chunk
    width = rext.shape[1] - (lags - 1)
    grouped = weight_bfloat.reshape(k_dev * groups, chunk, n_dev)
    dims = CONV_DIMS((0, 1, 2), (0, 2, 1), (0, 1, 2))
    partial = lax.conv_general_dilated(
        rext[None], grouped, (1,), [(0, 0)], dimension_numbers=dims,
        preferred_element_type=jnp.float32,
    )[0].reshape(k_dev, groups, -1)
    total = partial[:, 0, :width]
    for group in range(1, groups):
        total = total + partial[:, group, chunk * group : chunk * group + width]
    return total


def wnum_of(hext, ratio, piece=32):
    k_dev, length = hext.shape
    n_dev, width = ratio.shape
    lags = length - width + 1
    pieces = width // piece
    spans = -(-(lags + piece) // piece)
    pad = (pieces + spans) * piece - length
    folded = jnp.pad(hext, ((0, 0), (0, pad))).reshape(k_dev, pieces + spans, piece)
    lhs = jnp.concatenate([folded[:, i : i + pieces, :] for i in range(spans)], axis=2)
    rhs = ratio.reshape(n_dev, pieces, piece)
    dims = CONV_DIMS((0, 1, 2), (0, 1, 2), (0, 2, 1))
    out = lax.conv_general_dilated(
        lhs, rhs, (1,), [(0, 0)], dimension_numbers=dims,
        preferred_element_type=jnp.float32,
    )
    return out[:, :lags, :]


def local(counts, motif_w, motif_h):
    k_dev, lags, n_dev = motif_w.shape
    width = counts.shape[1]
    rim = lags - 1
    rows = k_dev * lags
    scale_factor = 1.0 / (MOTIFS * LAGS)
    total_bins = width * lax.axis_size("tm")
    leading_bin = lax.axis_index("tm") * width
    spike_events = counts.astype(jnp.float32)
    weights = motif_w.reshape(rows, n_dev)
    weight_bfloat = motif_w.astype(jnp.bfloat16)
    half_k = k_dev // 2
    second = lax.axis_index("tm") % 2 == 1
    mine = jnp.where(second, motif_w[half_k:], motif_w[:half_k]).astype(jnp.bfloat16)
    fetched = xor_swap(mine, "motif", 1)
    relayed = xor_swap(fetched, "tm", 1)
    partner_w = jnp.where(
        second,
        jnp.concatenate([relayed, fetched], axis=0),
        jnp.concatenate([fetched, relayed], axis=0),
    )
    weight_all = jnp.concatenate([weight_bfloat, partner_w], axis=0)
    acts = motif_h
    offset = scatter_offset("tm", rows)
    part_rows = rows // lax.axis_size("tm")
    def flip_lags(part):
        return jnp.flip(part.reshape(-1, lags, n_dev), axis=1).reshape(part.shape)

    weight_part = flip_lags(lax.dynamic_slice_in_dim(weights, offset, part_rows, axis=0))
    place = jnp.arange(width + rim, dtype=jnp.int32)[:, None]
    lag_ids = jnp.arange(lags, dtype=jnp.int32)[None, :]
    window = ((place >= lag_ids) & (place < lag_ids + width)).astype(jnp.bfloat16)

    def extend_padded(acts):
        hbf = acts.astype(jnp.bfloat16)
        tail = hbf[:, width - rim :]
        own = jnp.concatenate([from_behind(tail, "tm", 1), hbf], axis=1)
        other = jnp.concatenate(
            [from_behind_other(tail, 1), xor_swap(hbf, "motif", 1)], axis=1
        )
        return own, jnp.concatenate([own, other], axis=0)

    def ratio_of(weight_all, hext_all):
        estimated_counts = recon_of(weight_all, hext_all) * scale_factor
        return (spike_events / estimated_counts).astype(jnp.bfloat16)

    bins = leading_bin + jnp.arange(width, dtype=jnp.int32)
    offsets = jnp.arange(lags, dtype=jnp.int32)
    mask = (bins[None, :] + offsets[:, None] < total_bins).astype(jnp.float32)
    hext, hext_all = extend_padded(acts)
    for step in range(ITERS):
        ratio = ratio_of(weight_all, hext_all)
        after = from_behind(ratio[:, :rim], "tm", -1)
        inner = hnum_of(weight_bfloat, ratio)
        edge = hnum_of(weight_bfloat, jnp.concatenate([ratio[:, width - rim :], after], axis=1))
        hnum = jnp.concatenate([inner, edge], axis=1)
        colsum = jnp.sum(weight_bfloat, axis=2, dtype=jnp.float32)
        joined = neuron_sum(jnp.concatenate([hnum, colsum], axis=1))
        hnum, colsum = joined[:, :width], joined[:, width:]
        hden = jnp.dot(colsum, mask, precision=lax.Precision.HIGHEST)
        acts = acts * hnum / hden
        hext, hext_all = extend_padded(acts)
        ratio = ratio_of(weight_all, hext_all)
        wnum = wnum_of(hext, ratio).reshape(rows, n_dev)
        wden = jnp.dot(hext, window, preferred_element_type=jnp.float32).reshape(rows)
        blocks = lax.axis_size("tm")
        joined = jnp.concatenate(
            [wnum.reshape(blocks, part_rows, n_dev), wden.reshape(blocks, 1, part_rows)], axis=1
        )
        joined = sum_scatter(joined, "tm")[0]
        wnum, wden_part = joined[:part_rows], joined[part_rows]
        weight_part = weight_part * wnum / wden_part[:, None]
        if step + 1 < ITERS:
            part_bfloat = flip_lags(weight_part).astype(jnp.bfloat16)
            pair = jnp.stack([part_bfloat, xor_swap(part_bfloat, "motif", 1)], axis=0)
            pair = gather_rows(pair, "tm", dim=1)
            weight_all = pair.reshape(2 * k_dev, lags, n_dev)
            weight_bfloat = weight_all[:k_dev]
    weights = gather_rows(flip_lags(weight_part), "tm")
    return (weights.reshape(k_dev, lags, n_dev), acts)


def solution(mesh):
    in_specs = (P("neuron", "tm"), P("motif", None, "neuron"), P("motif", "tm"))
    out_specs = (P("motif", None, "neuron"), P("motif", "tm"))
    return jax.shard_map(local, mesh=mesh, in_specs=in_specs, out_specs=out_specs, check_vma=False)
```

```python
import jax
import jax.numpy as jnp
from jax import lax
from jax.sharding import PartitionSpec as P

MOTIFS = 64
LAGS = 64
ITERS = 2


def from_behind(value, axis, steps):
    count = lax.axis_size(axis)
    first, last = (max(0, -steps), min(count, count - steps))
    return lax.ppermute(value, axis, [(source, source + steps) for source in range(first, last)])


def xor_swap(value, axis, mask):
    count = lax.axis_size(axis)
    return lax.ppermute(value, axis, [(source, source ^ mask) for source in range(count)])


def masks_of(axis):
    count = lax.axis_size(axis)
    masks = []
    mask = 1
    while mask < count:
        masks.append(mask)
        mask *= 2
    return masks


def all_sum(value, axis):
    for mask in masks_of(axis):
        value = jax.tree.map(lambda a, b: a + b, value, xor_swap(value, axis, mask))
    return value


def ring_steps(axis):
    count = lax.axis_size(axis)
    if count != 8:
        return [
            ([source ^ mask for source in range(count)],
             [(source // mask) % 2 == 1 for source in range(count)])
            for mask in masks_of(axis)
        ]
    steps = [([source ^ 1 for source in range(8)], [source % 2 == 1 for source in range(8)])]
    for flip in (0, 1):
        partners, uppers = [], []
        for source in range(8):
            row, core = divmod(source, 2)
            if core == flip:
                other, upper = row ^ 1, row in (1, 2)
            else:
                other, upper = 3 - row, row in (2, 3)
            partners.append(2 * other + core)
            uppers.append(upper)
        steps.append((partners, uppers))
    return steps


def swap_with(value, axis, partners):
    return lax.ppermute(value, axis, [(source, target) for source, target in enumerate(partners)])


def upper_of(axis, uppers):
    return jnp.asarray(uppers)[lax.axis_index(axis)]


def sum_scatter(value, axis):
    for partners, uppers in ring_steps(axis):
        half = value.shape[0] // 2
        upper = upper_of(axis, uppers)
        send = lax.dynamic_slice_in_dim(value, jnp.where(upper, 0, half), half, axis=0)
        keep = lax.dynamic_slice_in_dim(value, jnp.where(upper, half, 0), half, axis=0)
        value = keep + swap_with(send, axis, partners)
    return value


def scatter_offset(axis, rows):
    offset = 0
    size = rows
    for partners, uppers in ring_steps(axis):
        size //= 2
        offset = offset + jnp.where(upper_of(axis, uppers), size, 0)
    return offset


def gather_rows(value, axis, dim=0):
    for partners, uppers in reversed(ring_steps(axis)):
        other = swap_with(value, axis, partners)
        upper = upper_of(axis, uppers)
        value = jnp.where(
            upper,
            jnp.concatenate([other, value], axis=dim),
            jnp.concatenate([value, other], axis=dim),
        )
    return value


def neuron_sum(value):
    count = lax.axis_size("neuron")
    rows = lax.axis_size("tm")
    if count != 8 or rows % 2:
        return all_sum(value, "neuron")
    value = value + xor_swap(value, "neuron", 1)
    for flip in (0, 1):
        pairs = []
        for row in range(rows):
            for source in range(count):
                ring, side = divmod(source, 2)
                other = ring ^ 1 if row % 2 == flip else 3 - ring
                pairs.append((row * count + source, row * count + 2 * other + side))
        value = value + lax.ppermute(value, ("tm", "neuron"), pairs)
    return value


def from_behind_other(value, steps):
    count = lax.axis_size("tm")
    pairs = [(2 * source + side, 2 * (source + steps) + 1 - side)
             for source in range(count - steps) for side in range(2)]
    return lax.ppermute(value, ("tm", "motif"), pairs)


CONV_DIMS = lax.ConvDimensionNumbers


def recon_of(weight_bfloat, hext):
    flipped = jnp.flip(weight_bfloat, axis=1)
    dims = CONV_DIMS((0, 1, 2), (2, 0, 1), (0, 1, 2))
    return lax.conv_general_dilated(
        hext[None], flipped, (1,), [(0, 0)], dimension_numbers=dims,
        preferred_element_type=jnp.float32,
    )[0]


def hnum_of(weight_bfloat, rext, chunk=16):
    k_dev, lags, n_dev = weight_bfloat.shape
    groups = lags // chunk
    width = rext.shape[1] - (lags - 1)
    grouped = weight_bfloat.reshape(k_dev * groups, chunk, n_dev)
    dims = CONV_DIMS((0, 1, 2), (0, 2, 1), (0, 1, 2))
    partial = lax.conv_general_dilated(
        rext[None], grouped, (1,), [(0, 0)], dimension_numbers=dims,
        preferred_element_type=jnp.float32,
    )[0].reshape(k_dev, groups, -1)
    total = partial[:, 0, :width]
    for group in range(1, groups):
        total = total + partial[:, group, chunk * group : chunk * group + width]
    return total


def wnum_of(hext, ratio, piece=64):
    k_dev, length = hext.shape
    n_dev, width = ratio.shape
    lags = length - width + 1
    pieces = width // piece
    spans = -(-(lags + piece) // piece)
    pad = (pieces + spans) * piece - length
    folded = jnp.pad(hext, ((0, 0), (0, pad))).reshape(k_dev, pieces + spans, piece)
    lhs = jnp.concatenate([folded[:, i : i + pieces, :] for i in range(spans)], axis=2)
    rhs = ratio.reshape(n_dev, pieces, piece)
    dims = CONV_DIMS((0, 1, 2), (0, 1, 2), (0, 2, 1))
    out = lax.conv_general_dilated(
        lhs, rhs, (1,), [(0, 0)], dimension_numbers=dims,
        preferred_element_type=jnp.float32,
    )
    return out[:, :lags, :]


def local(counts, motif_w, motif_h):
    k_dev, lags, n_dev = motif_w.shape
    width = counts.shape[1]
    rim = lags - 1
    rows = k_dev * lags
    scale_factor = 1.0 / (MOTIFS * LAGS)
    total_bins = width * lax.axis_size("tm")
    leading_bin = lax.axis_index("tm") * width
    spike_events = counts.astype(jnp.float32)
    weights = motif_w.reshape(rows, n_dev)
    weight_bfloat = motif_w.astype(jnp.bfloat16)
    half_k = k_dev // 2
    second = lax.axis_index("tm") % 2 == 1
    mine = jnp.where(second, weight_bfloat[half_k:], weight_bfloat[:half_k])
    fetched = xor_swap(mine, "motif", 1)
    relayed = xor_swap(fetched, "tm", 1)
    partner_w = jnp.where(
        second,
        jnp.concatenate([relayed, fetched], axis=0),
        jnp.concatenate([fetched, relayed], axis=0),
    )
    weight_all = jnp.concatenate([weight_bfloat, partner_w], axis=0)
    acts = motif_h
    offset = scatter_offset("tm", rows)
    part_rows = rows // lax.axis_size("tm")
    def flip_lags(part):
        return jnp.flip(part.reshape(-1, lags, n_dev), axis=1).reshape(part.shape)

    weight_part = flip_lags(lax.dynamic_slice_in_dim(weights, offset, part_rows, axis=0))
    place = jnp.arange(width + rim, dtype=jnp.int32)[:, None]
    lag_ids = jnp.arange(lags, dtype=jnp.int32)[None, :]
    window = ((place >= lag_ids) & (place < lag_ids + width)).astype(jnp.bfloat16)

    def extend_padded(acts):
        hbf = acts.astype(jnp.bfloat16)
        tail = hbf[:, width - rim :]
        own = jnp.concatenate([from_behind(tail, "tm", 1), hbf], axis=1)
        other = jnp.concatenate(
            [from_behind_other(tail, 1), xor_swap(hbf, "motif", 1)], axis=1
        )
        return own, jnp.concatenate([own, other], axis=0)

    def ratio_of(weight_all, hext_all):
        estimated_counts = recon_of(weight_all, hext_all) * scale_factor
        return (spike_events / estimated_counts).astype(jnp.bfloat16)

    bins = leading_bin + jnp.arange(width, dtype=jnp.int32)
    offsets = jnp.arange(lags, dtype=jnp.int32)
    mask = (bins[None, :] + offsets[:, None] < total_bins).astype(jnp.float32)
    hext, hext_all = extend_padded(acts)
    for step in range(ITERS):
        ratio = ratio_of(weight_all, hext_all)
        after = from_behind(ratio[:, :rim], "tm", -1)
        inner = hnum_of(weight_bfloat, ratio)
        edge = hnum_of(weight_bfloat, jnp.concatenate([ratio[:, width - rim :], after], axis=1))
        hnum = jnp.concatenate([inner, edge], axis=1)
        colsum = jnp.sum(weight_bfloat, axis=2, dtype=jnp.float32)
        joined = neuron_sum(jnp.concatenate([hnum, colsum], axis=1))
        hnum, colsum = joined[:, :width], joined[:, width:]
        hden = jnp.dot(colsum, mask, precision=lax.Precision.HIGHEST)
        acts = acts * hnum / hden
        hext, hext_all = extend_padded(acts)
        ratio = ratio_of(weight_all, hext_all)
        wnum = wnum_of(hext, ratio).reshape(rows, n_dev)
        wden = jnp.dot(hext, window, preferred_element_type=jnp.float32).reshape(rows)
        blocks = lax.axis_size("tm")
        joined = jnp.concatenate(
            [wnum.reshape(blocks, part_rows, n_dev), wden.reshape(blocks, 1, part_rows)], axis=1
        )
        joined = sum_scatter(joined, "tm")[0]
        wnum, wden_part = joined[:part_rows], joined[part_rows]
        weight_part = weight_part * wnum / wden_part[:, None]
        if step + 1 < ITERS:
            part_bfloat = flip_lags(weight_part).astype(jnp.bfloat16)
            pair = jnp.stack([part_bfloat, xor_swap(part_bfloat, "motif", 1)], axis=0)
            pair = gather_rows(pair, "tm", dim=1)
            weight_all = pair.reshape(2 * k_dev, lags, n_dev)
            weight_bfloat = weight_all[:k_dev]
    weights = gather_rows(flip_lags(weight_part), "tm")
    return (weights.reshape(k_dev, lags, n_dev), acts)


def solution(mesh):
    in_specs = (P("neuron", "tm"), P("motif", None, "neuron"), P("motif", "tm"))
    out_specs = (P("motif", None, "neuron"), P("motif", "tm"))
    return jax.shard_map(local, mesh=mesh, in_specs=in_specs, out_specs=out_specs, check_vma=False)
```

```python
import jax
import jax.numpy as jnp
from jax import lax
from jax.sharding import PartitionSpec as P

MOTIFS = 64
LAGS = 64
ITERS = 2


def from_behind(value, axis, steps):
    count = lax.axis_size(axis)
    first, last = (max(0, -steps), min(count, count - steps))
    return lax.ppermute(value, axis, [(source, source + steps) for source in range(first, last)])


def xor_swap(value, axis, mask):
    count = lax.axis_size(axis)
    return lax.ppermute(value, axis, [(source, source ^ mask) for source in range(count)])


def masks_of(axis):
    count = lax.axis_size(axis)
    masks = []
    mask = 1
    while mask < count:
        masks.append(mask)
        mask *= 2
    return masks


def all_sum(value, axis):
    for mask in masks_of(axis):
        value = jax.tree.map(lambda a, b: a + b, value, xor_swap(value, axis, mask))
    return value


def ring_steps(axis):
    count = lax.axis_size(axis)
    if count != 8:
        return [
            ([source ^ mask for source in range(count)],
             [(source // mask) % 2 == 1 for source in range(count)])
            for mask in masks_of(axis)
        ]
    steps = [([source ^ 1 for source in range(8)], [source % 2 == 1 for source in range(8)])]
    for flip in (0, 1):
        partners, uppers = [], []
        for source in range(8):
            row, core = divmod(source, 2)
            if core == flip:
                other, upper = row ^ 1, row in (1, 2)
            else:
                other, upper = 3 - row, row in (2, 3)
            partners.append(2 * other + core)
            uppers.append(upper)
        steps.append((partners, uppers))
    return steps


def swap_with(value, axis, partners):
    return lax.ppermute(value, axis, [(source, target) for source, target in enumerate(partners)])


def upper_of(axis, uppers):
    return jnp.asarray(uppers)[lax.axis_index(axis)]


def sum_scatter(value, axis):
    for partners, uppers in ring_steps(axis):
        half = value.shape[0] // 2
        upper = upper_of(axis, uppers)
        send = lax.dynamic_slice_in_dim(value, jnp.where(upper, 0, half), half, axis=0)
        keep = lax.dynamic_slice_in_dim(value, jnp.where(upper, half, 0), half, axis=0)
        value = keep + swap_with(send, axis, partners)
    return value


def scatter_offset(axis, rows):
    offset = 0
    size = rows
    for partners, uppers in ring_steps(axis):
        size //= 2
        offset = offset + jnp.where(upper_of(axis, uppers), size, 0)
    return offset


def gather_rows(value, axis, dim=0):
    for partners, uppers in reversed(ring_steps(axis)):
        other = swap_with(value, axis, partners)
        upper = upper_of(axis, uppers)
        value = jnp.where(
            upper,
            jnp.concatenate([other, value], axis=dim),
            jnp.concatenate([value, other], axis=dim),
        )
    return value


def neuron_sum(value):
    count = lax.axis_size("neuron")
    rows = lax.axis_size("tm")
    if count != 8 or rows % 2:
        return all_sum(value, "neuron")
    value = value + xor_swap(value, "neuron", 1)
    for flip in (0, 1):
        pairs = []
        for row in range(rows):
            for source in range(count):
                ring, side = divmod(source, 2)
                other = ring ^ 1 if row % 2 == flip else 3 - ring
                pairs.append((row * count + source, row * count + 2 * other + side))
        value = value + lax.ppermute(value, ("tm", "neuron"), pairs)
    return value


def from_behind_other(value, steps):
    count = lax.axis_size("tm")
    pairs = [(2 * source + side, 2 * (source + steps) + 1 - side)
             for source in range(count - steps) for side in range(2)]
    return lax.ppermute(value, ("tm", "motif"), pairs)


CONV_DIMS = lax.ConvDimensionNumbers


def recon_of(weight_bfloat, hext):
    flipped = jnp.flip(weight_bfloat, axis=1)
    dims = CONV_DIMS((0, 1, 2), (2, 0, 1), (0, 1, 2))
    return lax.conv_general_dilated(
        hext[None], flipped, (1,), [(0, 0)], dimension_numbers=dims,
        preferred_element_type=jnp.float32,
    )[0]


def hnum_of(weight_bfloat, rext, chunk=32):
    k_dev, lags, n_dev = weight_bfloat.shape
    groups = lags // chunk
    width = rext.shape[1] - (lags - 1)
    grouped = weight_bfloat.reshape(k_dev * groups, chunk, n_dev)
    dims = CONV_DIMS((0, 1, 2), (0, 2, 1), (0, 1, 2))
    partial = lax.conv_general_dilated(
        rext[None], grouped, (1,), [(0, 0)], dimension_numbers=dims,
        preferred_element_type=jnp.float32,
    )[0].reshape(k_dev, groups, -1)
    total = partial[:, 0, :width]
    for group in range(1, groups):
        total = total + partial[:, group, chunk * group : chunk * group + width]
    return total


def wnum_of(hext, ratio, piece=32):
    k_dev, length = hext.shape
    n_dev, width = ratio.shape
    lags = length - width + 1
    pieces = width // piece
    spans = -(-(lags + piece) // piece)
    pad = (pieces + spans) * piece - length
    folded = jnp.pad(hext, ((0, 0), (0, pad))).reshape(k_dev, pieces + spans, piece)
    lhs = jnp.concatenate([folded[:, i : i + pieces, :] for i in range(spans)], axis=2)
    rhs = ratio.reshape(n_dev, pieces, piece)
    dims = CONV_DIMS((0, 1, 2), (0, 1, 2), (0, 2, 1))
    out = lax.conv_general_dilated(
        lhs, rhs, (1,), [(0, 0)], dimension_numbers=dims,
        preferred_element_type=jnp.float32,
    )
    return out[:, :lags, :]


def local(counts, motif_w, motif_h):
    k_dev, lags, n_dev = motif_w.shape
    width = counts.shape[1]
    rim = lags - 1
    rows = k_dev * lags
    scale_factor = 1.0 / (MOTIFS * LAGS)
    total_bins = width * lax.axis_size("tm")
    leading_bin = lax.axis_index("tm") * width
    spike_events = counts.astype(jnp.float32)
    weights = motif_w.reshape(rows, n_dev)
    weight_bfloat = motif_w.astype(jnp.bfloat16)
    half_k = k_dev // 2
    second = lax.axis_index("tm") % 2 == 1
    mine = jnp.where(second, weight_bfloat[half_k:], weight_bfloat[:half_k])
    fetched = xor_swap(mine, "motif", 1)
    relayed = xor_swap(fetched, "tm", 1)
    partner_w = jnp.where(
        second,
        jnp.concatenate([relayed, fetched], axis=0),
        jnp.concatenate([fetched, relayed], axis=0),
    )
    weight_all = jnp.concatenate([weight_bfloat, partner_w], axis=0)
    acts = motif_h
    offset = scatter_offset("tm", rows)
    part_rows = rows // lax.axis_size("tm")
    def flip_lags(part):
        return jnp.flip(part.reshape(-1, lags, n_dev), axis=1).reshape(part.shape)

    weight_part = flip_lags(lax.dynamic_slice_in_dim(weights, offset, part_rows, axis=0))
    place = jnp.arange(width + rim, dtype=jnp.int32)[:, None]
    lag_ids = jnp.arange(lags, dtype=jnp.int32)[None, :]
    window = ((place >= lag_ids) & (place < lag_ids + width)).astype(jnp.bfloat16)

    def extend_padded(acts):
        hbf = acts.astype(jnp.bfloat16)
        tail = hbf[:, width - rim :]
        own = jnp.concatenate([from_behind(tail, "tm", 1), hbf], axis=1)
        other = jnp.concatenate(
            [from_behind_other(tail, 1), xor_swap(hbf, "motif", 1)], axis=1
        )
        return own, jnp.concatenate([own, other], axis=0)

    def ratio_of(weight_all, hext_all):
        estimated_counts = recon_of(weight_all, hext_all) * scale_factor
        return (spike_events / estimated_counts).astype(jnp.bfloat16)

    bins = leading_bin + jnp.arange(width, dtype=jnp.int32)
    offsets = jnp.arange(lags, dtype=jnp.int32)
    mask = (bins[None, :] + offsets[:, None] < total_bins).astype(jnp.float32)
    hext, hext_all = extend_padded(acts)
    for step in range(ITERS):
        ratio = ratio_of(weight_all, hext_all)
        after = from_behind(ratio[:, :rim], "tm", -1)
        inner = hnum_of(weight_bfloat, ratio)
        edge = hnum_of(weight_bfloat, jnp.concatenate([ratio[:, width - rim :], after], axis=1))
        hnum = jnp.concatenate([inner, edge], axis=1)
        colsum = jnp.sum(weight_bfloat, axis=2, dtype=jnp.float32)
        joined = neuron_sum(jnp.concatenate([hnum, colsum], axis=1))
        hnum, colsum = joined[:, :width], joined[:, width:]
        hden = jnp.dot(colsum, mask, precision=lax.Precision.HIGHEST)
        acts = acts * hnum / hden
        hext, hext_all = extend_padded(acts)
        ratio = ratio_of(weight_all, hext_all)
        wnum = wnum_of(hext, ratio).reshape(rows, n_dev)
        wden = jnp.dot(hext, window, preferred_element_type=jnp.float32).reshape(rows)
        blocks = lax.axis_size("tm")
        joined = jnp.concatenate(
            [wnum.reshape(blocks, part_rows, n_dev), wden.reshape(blocks, 1, part_rows)], axis=1
        )
        joined = sum_scatter(joined, "tm")[0]
        wnum, wden_part = joined[:part_rows], joined[part_rows]
        weight_part = weight_part * wnum / wden_part[:, None]
        if step + 1 < ITERS:
            part_bfloat = flip_lags(weight_part).astype(jnp.bfloat16)
            pair = jnp.stack([part_bfloat, xor_swap(part_bfloat, "motif", 1)], axis=0)
            pair = gather_rows(pair, "tm", dim=1)
            weight_all = pair.reshape(2 * k_dev, lags, n_dev)
            weight_bfloat = weight_all[:k_dev]
    weights = gather_rows(flip_lags(weight_part), "tm")
    return (weights.reshape(k_dev, lags, n_dev), acts)


def solution(mesh):
    in_specs = (P("neuron", "tm"), P("motif", None, "neuron"), P("motif", "tm"))
    out_specs = (P("motif", None, "neuron"), P("motif", "tm"))
    return jax.shard_map(local, mesh=mesh, in_specs=in_specs, out_specs=out_specs, check_vma=False)
```

```python
import jax
import jax.numpy as jnp
from jax import lax
from jax.sharding import PartitionSpec as P

MOTIFS = 64
LAGS = 64
ITERS = 2


def from_behind(value, axis, steps):
    count = lax.axis_size(axis)
    first, last = (max(0, -steps), min(count, count - steps))
    return lax.ppermute(value, axis, [(source, source + steps) for source in range(first, last)])


def xor_swap(value, axis, mask):
    count = lax.axis_size(axis)
    return lax.ppermute(value, axis, [(source, source ^ mask) for source in range(count)])


def masks_of(axis):
    count = lax.axis_size(axis)
    masks = []
    mask = 1
    while mask < count:
        masks.append(mask)
        mask *= 2
    return masks


def all_sum(value, axis):
    for mask in masks_of(axis):
        value = jax.tree.map(lambda a, b: a + b, value, xor_swap(value, axis, mask))
    return value


def ring_steps(axis):
    count = lax.axis_size(axis)
    if count != 8:
        return [
            ([source ^ mask for source in range(count)],
             [(source // mask) % 2 == 1 for source in range(count)])
            for mask in masks_of(axis)
        ]
    steps = [([source ^ 1 for source in range(8)], [source % 2 == 1 for source in range(8)])]
    for flip in (0, 1):
        partners, uppers = [], []
        for source in range(8):
            row, core = divmod(source, 2)
            if core == flip:
                other, upper = row ^ 1, row in (1, 2)
            else:
                other, upper = 3 - row, row in (2, 3)
            partners.append(2 * other + core)
            uppers.append(upper)
        steps.append((partners, uppers))
    return steps


def swap_with(value, axis, partners):
    return lax.ppermute(value, axis, [(source, target) for source, target in enumerate(partners)])


def upper_of(axis, uppers):
    return jnp.asarray(uppers)[lax.axis_index(axis)]


def sum_scatter(value, axis):
    for partners, uppers in ring_steps(axis):
        half = value.shape[0] // 2
        upper = upper_of(axis, uppers)
        send = lax.dynamic_slice_in_dim(value, jnp.where(upper, 0, half), half, axis=0)
        keep = lax.dynamic_slice_in_dim(value, jnp.where(upper, half, 0), half, axis=0)
        value = keep + swap_with(send, axis, partners)
    return value


def scatter_offset(axis, rows):
    offset = 0
    size = rows
    for partners, uppers in ring_steps(axis):
        size //= 2
        offset = offset + jnp.where(upper_of(axis, uppers), size, 0)
    return offset


def gather_rows(value, axis, dim=0):
    for partners, uppers in reversed(ring_steps(axis)):
        other = swap_with(value, axis, partners)
        upper = upper_of(axis, uppers)
        value = jnp.where(
            upper,
            jnp.concatenate([other, value], axis=dim),
            jnp.concatenate([value, other], axis=dim),
        )
    return value


def neuron_sum(value):
    count = lax.axis_size("neuron")
    rows = lax.axis_size("tm")
    if count != 8 or rows % 2:
        return all_sum(value, "neuron")
    for flip in (0, 1):
        pairs = []
        for row in range(rows):
            for source in range(count):
                ring, side = divmod(source, 2)
                other = ring ^ 1 if row % 2 == flip else 3 - ring
                pairs.append((row * count + source, row * count + 2 * other + side))
        value = value + lax.ppermute(value, ("tm", "neuron"), pairs)
    return value + xor_swap(value, "neuron", 1)


def from_behind_other(value, steps):
    count = lax.axis_size("tm")
    pairs = [(2 * source + side, 2 * (source + steps) + 1 - side)
             for source in range(count - steps) for side in range(2)]
    return lax.ppermute(value, ("tm", "motif"), pairs)


CONV_DIMS = lax.ConvDimensionNumbers


def recon_of(weight_bfloat, hext):
    flipped = jnp.flip(weight_bfloat, axis=1)
    dims = CONV_DIMS((0, 1, 2), (2, 0, 1), (0, 1, 2))
    return lax.conv_general_dilated(
        hext[None], flipped, (1,), [(0, 0)], dimension_numbers=dims,
        preferred_element_type=jnp.float32,
    )[0]


def hnum_of(weight_bfloat, rext, chunk=16):
    k_dev, lags, n_dev = weight_bfloat.shape
    groups = lags // chunk
    width = rext.shape[1] - (lags - 1)
    grouped = weight_bfloat.reshape(k_dev * groups, chunk, n_dev)
    dims = CONV_DIMS((0, 1, 2), (0, 2, 1), (0, 1, 2))
    partial = lax.conv_general_dilated(
        rext[None], grouped, (1,), [(0, 0)], dimension_numbers=dims,
        preferred_element_type=jnp.float32,
    )[0].reshape(k_dev, groups, -1)
    total = partial[:, 0, :width]
    for group in range(1, groups):
        total = total + partial[:, group, chunk * group : chunk * group + width]
    return total


def wnum_of(hext, ratio, piece=32):
    k_dev, length = hext.shape
    n_dev, width = ratio.shape
    lags = length - width + 1
    pieces = width // piece
    spans = -(-(lags + piece) // piece)
    pad = (pieces + spans) * piece - length
    folded = jnp.pad(hext, ((0, 0), (0, pad))).reshape(k_dev, pieces + spans, piece)
    lhs = jnp.concatenate([folded[:, i : i + pieces, :] for i in range(spans)], axis=2)
    rhs = ratio.reshape(n_dev, pieces, piece)
    dims = CONV_DIMS((0, 1, 2), (0, 1, 2), (0, 2, 1))
    out = lax.conv_general_dilated(
        lhs, rhs, (1,), [(0, 0)], dimension_numbers=dims,
        preferred_element_type=jnp.float32,
    )
    return out[:, :lags, :]


def local(counts, motif_w, motif_h):
    k_dev, lags, n_dev = motif_w.shape
    width = counts.shape[1]
    rim = lags - 1
    rows = k_dev * lags
    scale_factor = 1.0 / (MOTIFS * LAGS)
    total_bins = width * lax.axis_size("tm")
    leading_bin = lax.axis_index("tm") * width
    spike_events = counts.astype(jnp.float32)
    weights = motif_w.reshape(rows, n_dev)
    weight_bfloat = motif_w.astype(jnp.bfloat16)
    half_k = k_dev // 2
    second = lax.axis_index("tm") % 2 == 1
    mine = jnp.where(second, weight_bfloat[half_k:], weight_bfloat[:half_k])
    fetched = xor_swap(mine, "motif", 1)
    relayed = xor_swap(fetched, "tm", 1)
    partner_w = jnp.where(
        second,
        jnp.concatenate([relayed, fetched], axis=0),
        jnp.concatenate([fetched, relayed], axis=0),
    )
    weight_all = jnp.concatenate([weight_bfloat, partner_w], axis=0)
    acts = motif_h
    offset = scatter_offset("tm", rows)
    part_rows = rows // lax.axis_size("tm")
    def flip_lags(part):
        return jnp.flip(part.reshape(-1, lags, n_dev), axis=1).reshape(part.shape)

    weight_part = flip_lags(lax.dynamic_slice_in_dim(weights, offset, part_rows, axis=0))
    place = jnp.arange(width + rim, dtype=jnp.int32)[:, None]
    lag_ids = jnp.arange(lags, dtype=jnp.int32)[None, :]
    window = ((place >= lag_ids) & (place < lag_ids + width)).astype(jnp.bfloat16)

    def extend_padded(acts):
        hbf = acts.astype(jnp.bfloat16)
        tail = hbf[:, width - rim :]
        own = jnp.concatenate([from_behind(tail, "tm", 1), hbf], axis=1)
        other = jnp.concatenate(
            [from_behind_other(tail, 1), xor_swap(hbf, "motif", 1)], axis=1
        )
        return own, jnp.concatenate([own, other], axis=0)

    def ratio_of(weight_all, hext_all):
        estimated_counts = recon_of(weight_all, hext_all) * scale_factor
        return (spike_events / estimated_counts).astype(jnp.bfloat16)

    bins = leading_bin + jnp.arange(width, dtype=jnp.int32)
    offsets = jnp.arange(lags, dtype=jnp.int32)
    mask = (bins[None, :] + offsets[:, None] < total_bins).astype(jnp.float32)
    hext, hext_all = extend_padded(acts)
    for step in range(ITERS):
        ratio = ratio_of(weight_all, hext_all)
        after = from_behind(ratio[:, :rim], "tm", -1)
        inner = hnum_of(weight_bfloat, ratio)
        edge = hnum_of(weight_bfloat, jnp.concatenate([ratio[:, width - rim :], after], axis=1))
        hnum = jnp.concatenate([inner, edge], axis=1)
        colsum = jnp.sum(weight_bfloat, axis=2, dtype=jnp.float32)
        joined = neuron_sum(jnp.concatenate([hnum, colsum], axis=1))
        hnum, colsum = joined[:, :width], joined[:, width:]
        hden = jnp.dot(colsum, mask, precision=lax.Precision.HIGHEST)
        acts = acts * hnum / hden
        hext, hext_all = extend_padded(acts)
        ratio = ratio_of(weight_all, hext_all)
        wnum = wnum_of(hext, ratio).reshape(rows, n_dev)
        wden = jnp.dot(hext, window, preferred_element_type=jnp.float32).reshape(rows)
        blocks = lax.axis_size("tm")
        joined = jnp.concatenate(
            [wnum.reshape(blocks, part_rows, n_dev), wden.reshape(blocks, 1, part_rows)], axis=1
        )
        joined = sum_scatter(joined, "tm")[0]
        wnum, wden_part = joined[:part_rows], joined[part_rows]
        weight_part = weight_part * wnum / wden_part[:, None]
        if step + 1 < ITERS:
            part_bfloat = flip_lags(weight_part).astype(jnp.bfloat16)
            pair = jnp.stack([part_bfloat, xor_swap(part_bfloat, "motif", 1)], axis=0)
            pair = gather_rows(pair, "tm", dim=1)
            weight_all = pair.reshape(2 * k_dev, lags, n_dev)
            weight_bfloat = weight_all[:k_dev]
    weights = gather_rows(flip_lags(weight_part), "tm")
    return (weights.reshape(k_dev, lags, n_dev), acts)


def solution(mesh):
    in_specs = (P("neuron", "tm"), P("motif", None, "neuron"), P("motif", "tm"))
    out_specs = (P("motif", None, "neuron"), P("motif", "tm"))
    return jax.shard_map(local, mesh=mesh, in_specs=in_specs, out_specs=out_specs, check_vma=False)
```
